32 devices in a mesh: seq: 8 (over z, core), chan: 4 (over y, x).
Axes of the slice: x: 2, y: 2, z: 4, core: 2. Of those that a mesh axis runs over, the one named last changes fastest.
Arguments:
- grad_out: bfloat16 [4096, 8192], P('seq', 'chan'), may hold values from -6 to 6
- qkv_saved: bfloat16 [4096, 3, 8192], P('seq', None, 'chan'), may hold values from -6 to 6
- conv_saved: bfloat16 [4096, 8192], P('seq', 'chan'), may hold values from -6 to 6
- long_taps: bfloat16 [4096, 512], P('seq', 'chan'), may hold values from -1 to 1
- short_taps: float32 [3, 3, 8192], P(None, None, 'chan'), may hold values from -3 to 3
Outputs:
- grad_proj: bfloat16 [4096, 3, 8192], P(('seq', 'chan'))
The draws below stay inside these ranges and needn't reach their ends.
All inputs are finite; a program needn't handle non-finite values.
Results may differ from the reference program's by a relative error of at most 0.0042.
Values may be sent and summed in bfloat16 or wider, within the bound.
No kernel may reach another device: no remote copies, remote signals or barrier semaphores. Data moves between devices by JAX's collectives and lax.ppermute only.
A program may use at most 128 MiB of HBM per device.

```python
import math
import jax
import jax.numpy as jnp
from jax import lax

D = 8192
GROUP = 16
SHORT = 3
TOKENS = 4096
GROUPS = 512


def draw_long_taps(key, part):
    key_tau, key_noise = jax.random.split(jax.random.fold_in(key, 7))
    lags = jnp.arange(TOKENS, dtype=jnp.float32)[:, None]
    log_tau = jax.random.uniform(key_tau, (1, GROUPS), jnp.float32, math.log(32.0), math.log(4 * TOKENS))
    noise = jnp.clip(jax.random.normal(key_noise, (TOKENS, GROUPS), jnp.float32), -4.0, 4.0)
    decay = jnp.exp(log_tau)
    spread = jnp.sqrt(2.0 / jnp.minimum(decay, float(TOKENS)))
    return (noise * spread * jnp.exp(-lags / decay)).astype(jnp.bfloat16)


def levels(own_key, extent, cuts, smallest, top_value):
    level = 1.0
    for dim, shards_of in cuts:
        heights = jax.random.uniform(jax.random.fold_in(jax.random.fold_in(own_key, 6), dim), (shards_of,), jnp.float32, smallest / len(cuts), top_value / len(cuts))
        level = level * jnp.repeat(jnp.exp(heights), extent[dim] // shards_of).reshape((-1,) + (1,) * (len(extent) - 1 - dim))
    return level


def centred(stream_key, dims, width, bound, cuts=(), kind=jnp.bfloat16):
    values = jax.random.normal(stream_key, dims, jnp.float32) * width
    if len(cuts) > 0:
        values = levels(stream_key, dims, cuts, -0.22, 0.18) * values
    return jnp.clip(values, min=-bound, max=bound).astype(kind)


def setup_inputs(seed: int = 0) -> dict:
    arg_keys = jax.random.split(jax.random.key(seed), 6)
    grad_out = centred(arg_keys[0], (TOKENS, D), 1.0, 6.0, ((0, 8), (1, 4)))
    qkv_saved = centred(arg_keys[1], (TOKENS, 3, D), 1.0, 6.0, ((0, 8), (2, 4)))
    conv_saved = centred(arg_keys[2], (TOKENS, D), 1.0, 6.0, ((0, 8), (1, 4)))
    long_taps = draw_long_taps(jax.random.fold_in(arg_keys[5], 71), 0)
    short_taps = centred(arg_keys[4], (3, SHORT, D), 0.6, 3.0, ((2, 4),), jnp.float32)
    return {"grad_out": grad_out, "qkv_saved": qkv_saved, "conv_saved": conv_saved, "long_taps": long_taps, "short_taps": short_taps}


def correlate_block(pair):
    grads, filters = pair
    length = grads.shape[0]
    reverse = grads[::-1]
    spectrum = jnp.fft.rfft(filters, 2 * length, axis=0) * jnp.fft.rfft(reverse, 2 * length, axis=0)
    return jnp.fft.irfft(spectrum, 2 * length, axis=0)[:length][::-1]


def reference(grad_out, qkv_saved, conv_saved, long_taps, short_taps):
    out_wide = grad_out.astype(jnp.float32)
    query = qkv_saved[:, 0, :].astype(jnp.float32)
    key_part = qkv_saved[:, 1, :].astype(jnp.float32)
    value_part = qkv_saved[:, 2, :].astype(jnp.float32)
    grad_query = out_wide * conv_saved.astype(jnp.float32)
    grad_mixed = lax.optimization_barrier((out_wide * query).astype(jnp.bfloat16)).astype(jnp.float32)
    filters = jnp.repeat(long_taps.astype(jnp.float32), GROUP, axis=1)
    blocks = 8
    piece = D // blocks
    grads_split = grad_mixed.reshape(TOKENS, blocks, piece).transpose(1, 0, 2)
    filters_split = filters.reshape(TOKENS, blocks, piece).transpose(1, 0, 2)
    grad_z = lax.map(correlate_block, (grads_split, filters_split))
    grad_z = grad_z.transpose(1, 0, 2).reshape(TOKENS, D)
    grad_key = grad_z * value_part
    grad_value = grad_z * key_part
    stacked = jnp.stack([grad_query, grad_key, grad_value], 1)
    extended = jnp.concatenate([stacked, jnp.zeros((SHORT - 1, 3, D), stacked.dtype)], 0)
    result = jnp.zeros_like(stacked)
    for lag_index in range(SHORT):
        result = result + short_taps[:, lag_index, :][None] * extended[lag_index:lag_index + TOKENS]
    return result.astype(jnp.bfloat16)
```

```python
import functools

import jax
import jax.numpy as jnp
from jax import lax
from jax.experimental import pallas as pl
from jax.experimental.pallas import tpu as pltpu
from jax.sharding import PartitionSpec as P

block = 256
per_group = 16


def shifted(value, axis, steps):
    count = lax.axis_size(axis)
    leading, last = (max(0, -steps), min(count, count - steps))
    return lax.ppermute(value, axis, [(source, source + steps) for source in range(leading, last)])


def correlate_kernel(x_ref, h_ref, o_ref):
    rows_all = x_ref.shape[1]
    blocks = rows_all // per_group
    tokens = blocks * block
    o_ref[...] = jnp.zeros(o_ref.shape, o_ref.dtype)
    for lag_block in range(blocks):
        start = tokens - block * (lag_block + 1)
        window = h_ref[0, :, start : start + 2 * block]
        spread = jnp.broadcast_to(window, (block, 2 * block))
        rolled = pltpu.roll(spread, block + 1, 1, stride=1, stride_axis=0)
        band = rolled[:, :block].astype(jnp.bfloat16)
        rows = per_group * (blocks - lag_block)
        source = x_ref[0, per_group * lag_block :, :]
        o_ref[0, :rows, :] += jnp.dot(source, band, preferred_element_type=jnp.float32)


def correlate(grads, taps):
    tokens, channels = grads.shape
    groups = taps.shape[1]
    blocks = tokens // block
    shaped = grads.reshape(blocks, block, groups, per_group).transpose(2, 0, 3, 1)
    shaped = shaped.reshape(groups, blocks * per_group, block)
    reversed_taps = taps.astype(jnp.float32).T[:, ::-1]
    padded = jnp.concatenate([reversed_taps, jnp.zeros((groups, block), jnp.float32)], 1)
    padded = padded.reshape(groups, 1, tokens + block)
    flops = 2 * groups * per_group * block * block * blocks * (blocks + 1) // 2
    out = pl.pallas_call(
        correlate_kernel,
        out_shape=jax.ShapeDtypeStruct((groups, blocks * per_group, block), jnp.float32),
        grid=(groups,),
        in_specs=[
            pl.BlockSpec((1, blocks * per_group, block), lambda g: (g, 0, 0)),
            pl.BlockSpec((1, 1, tokens + block), lambda g: (g, 0, 0)),
        ],
        out_specs=pl.BlockSpec((1, blocks * per_group, block), lambda g: (g, 0, 0)),
        cost_estimate=pl.CostEstimate(
            flops=flops, bytes_accessed=grads.size * 6 + padded.size * 4, transcendentals=0
        ),
    )(shaped, padded)
    out = out.reshape(groups, blocks, per_group, block).transpose(1, 3, 0, 2)
    return out.reshape(tokens, channels)


def on_device(grad_out, qkv_saved, conv_saved, long_taps, short_taps):
    block_rows = grad_out.shape[0]
    out_wide = grad_out.astype(jnp.float32)
    query = qkv_saved[:, 0, :]
    key_part = qkv_saved[:, 1, :]
    value_part = qkv_saved[:, 2, :]
    grad_query = out_wide * conv_saved.astype(jnp.float32)
    grad_mixed = (out_wide * query.astype(jnp.float32)).astype(jnp.bfloat16)
    mixed_cols = lax.all_to_all(grad_mixed, "seq", split_axis=1, concat_axis=0, tiled=True)
    taps_cols = lax.all_to_all(long_taps, "seq", split_axis=1, concat_axis=0, tiled=True)
    z_cols = correlate(mixed_cols, taps_cols)
    grad_z = lax.all_to_all(z_cols, "seq", split_axis=0, concat_axis=1, tiled=True)
    grad_key = grad_z * value_part.astype(jnp.float32)
    grad_value = grad_z * key_part.astype(jnp.float32)
    stacked = jnp.stack([grad_query, grad_key, grad_value], 1)
    short_len = short_taps.shape[1]
    borrowed = shifted(stacked[: short_len - 1], "seq", -1)
    extended = jnp.concatenate([stacked, borrowed], 0)
    result = jnp.zeros_like(stacked)
    for lag_index in range(short_len):
        result = (
            result
            + short_taps[:, lag_index, :][None] * extended[lag_index : lag_index + block_rows]
        )
    mixed = result.astype(jnp.bfloat16)
    return lax.all_to_all(mixed, "chan", split_axis=0, concat_axis=2, tiled=True)


def solution(mesh):
    in_specs = (
        P("seq", "chan"),
        P("seq", None, "chan"),
        P("seq", "chan"),
        P("seq", "chan"),
        P(None, None, "chan"),
    )
    out_specs = P(("seq", "chan"), None, None)
    return jax.shard_map(
        on_device, mesh=mesh, in_specs=in_specs, out_specs=out_specs, check_vma=False
    )
```

```python
import functools

import jax
import jax.numpy as jnp
from jax import lax
from jax.experimental import pallas as pl
from jax.experimental.pallas import tpu as pltpu
from jax.sharding import PartitionSpec as P

block = 256
per_group = 16


def shifted(value, axis, steps):
    count = lax.axis_size(axis)
    leading, last = (max(0, -steps), min(count, count - steps))
    return lax.ppermute(value, axis, [(source, source + steps) for source in range(leading, last)])


def correlate_kernel(x_ref, h_ref, o_ref):
    rows_all = x_ref.shape[1]
    blocks = rows_all // per_group
    tokens = blocks * block
    o_ref[...] = jnp.zeros(o_ref.shape, o_ref.dtype)
    for lag_block in range(blocks):
        start = tokens - block * (lag_block + 1)
        window = h_ref[0, :, start : start + 2 * block]
        spread = jnp.broadcast_to(window, (block, 2 * block))
        rolled = pltpu.roll(spread, block + 1, 1, stride=1, stride_axis=0)
        band = rolled[:, :block].astype(jnp.bfloat16)
        rows = per_group * (blocks - lag_block)
        source = x_ref[0, per_group * lag_block :, :]
        o_ref[0, :rows, :] += jnp.dot(source, band, preferred_element_type=jnp.float32)


def correlate(grads, taps):
    tokens, channels = grads.shape
    groups = taps.shape[1]
    blocks = tokens // block
    shaped = grads.reshape(blocks, block, groups, per_group).transpose(2, 0, 3, 1)
    shaped = shaped.reshape(groups, blocks * per_group, block)
    reversed_taps = taps.astype(jnp.float32).T[:, ::-1]
    padded = jnp.concatenate([reversed_taps, jnp.zeros((groups, block), jnp.float32)], 1)
    padded = padded.reshape(groups, 1, tokens + block)
    flops = 2 * groups * per_group * block * block * blocks * (blocks + 1) // 2
    out = pl.pallas_call(
        correlate_kernel,
        out_shape=jax.ShapeDtypeStruct((groups, blocks * per_group, block), jnp.float32),
        grid=(groups,),
        in_specs=[
            pl.BlockSpec((1, blocks * per_group, block), lambda g: (g, 0, 0)),
            pl.BlockSpec((1, 1, tokens + block), lambda g: (g, 0, 0)),
        ],
        out_specs=pl.BlockSpec((1, blocks * per_group, block), lambda g: (g, 0, 0)),
        cost_estimate=pl.CostEstimate(
            flops=flops, bytes_accessed=grads.size * 6 + padded.size * 4, transcendentals=0
        ),
    )(shaped, padded)
    out = out.reshape(groups, blocks, per_group, block).transpose(1, 3, 0, 2)
    return out.reshape(tokens, channels)


def on_device(grad_out, qkv_saved, conv_saved, long_taps, short_taps):
    block_rows = grad_out.shape[0]
    out_wide = grad_out.astype(jnp.float32)
    query = qkv_saved[:, 0, :]
    key_part = qkv_saved[:, 1, :]
    value_part = qkv_saved[:, 2, :]
    grad_query = out_wide * conv_saved.astype(jnp.float32)
    grad_mixed = (out_wide * query.astype(jnp.float32)).astype(jnp.bfloat16)
    mixed_cols = lax.all_to_all(grad_mixed, "seq", split_axis=1, concat_axis=0, tiled=True)
    taps_cols = lax.all_to_all(long_taps, "seq", split_axis=1, concat_axis=0, tiled=True)
    short_len = short_taps.shape[1]
    query_proj = short_filter(grad_query[:, None], short_taps[:1], block_rows)
    query_rows = lax.all_to_all(query_proj, "chan", split_axis=0, concat_axis=2, tiled=True)
    z_cols = correlate(mixed_cols, taps_cols)
    grad_z = lax.all_to_all(z_cols, "seq", split_axis=0, concat_axis=1, tiled=True)
    grad_key = grad_z * value_part.astype(jnp.float32)
    grad_value = grad_z * key_part.astype(jnp.float32)
    stacked = jnp.stack([grad_key, grad_value], 1)
    pair_proj = short_filter(stacked, short_taps[1:], block_rows)
    pair_rows = lax.all_to_all(pair_proj, "chan", split_axis=0, concat_axis=2, tiled=True)
    return jnp.concatenate([query_rows, pair_rows], 1)


def short_filter(stacked, taps, block_rows):
    short_len = taps.shape[1]
    borrowed = shifted(stacked[: short_len - 1], "seq", -1)
    extended = jnp.concatenate([stacked, borrowed], 0)
    result = jnp.zeros_like(stacked)
    for lag_index in range(short_len):
        result = result + taps[:, lag_index, :][None] * extended[lag_index : lag_index + block_rows]
    return result.astype(jnp.bfloat16)


def solution(mesh):
    in_specs = (
        P("seq", "chan"),
        P("seq", None, "chan"),
        P("seq", "chan"),
        P("seq", "chan"),
        P(None, None, "chan"),
    )
    out_specs = P(("seq", "chan"), None, None)
    return jax.shard_map(
        on_device, mesh=mesh, in_specs=in_specs, out_specs=out_specs, check_vma=False
    )
```

```python
import functools

import jax
import jax.numpy as jnp
from jax import lax
from jax.experimental import pallas as pl
from jax.experimental.pallas import tpu as pltpu
from jax.sharding import PartitionSpec as P

block = 256
per_group = 16


def shifted(value, axis, steps):
    count = lax.axis_size(axis)
    leading, last = (max(0, -steps), min(count, count - steps))
    return lax.ppermute(value, axis, [(source, source + steps) for source in range(leading, last)])


def correlate_kernel(x_ref, h_ref, o_ref):
    rows_all = x_ref.shape[1]
    blocks = rows_all // per_group
    tokens = blocks * block
    o_ref[...] = jnp.zeros(o_ref.shape, o_ref.dtype)
    for lag_block in range(blocks):
        start = tokens - block * (lag_block + 1)
        window = h_ref[0, :, start : start + 2 * block]
        spread = jnp.broadcast_to(window, (block, 2 * block))
        rolled = pltpu.roll(spread, block + 1, 1, stride=1, stride_axis=0)
        band = rolled[:, :block].astype(jnp.bfloat16)
        rows = per_group * (blocks - lag_block)
        source = x_ref[0, per_group * lag_block :, :]
        o_ref[0, :rows, :] += jnp.dot(source, band, preferred_element_type=jnp.float32)


def correlate(grads, taps):
    tokens, channels = grads.shape
    groups = taps.shape[1]
    blocks = tokens // block
    shaped = grads.reshape(blocks, block, groups, per_group).transpose(2, 0, 3, 1)
    shaped = shaped.reshape(groups, blocks * per_group, block)
    reversed_taps = taps.astype(jnp.float32).T[:, ::-1]
    padded = jnp.concatenate([reversed_taps, jnp.zeros((groups, block), jnp.float32)], 1)
    padded = padded.reshape(groups, 1, tokens + block)
    flops = 2 * groups * per_group * block * block * blocks * (blocks + 1) // 2
    out = pl.pallas_call(
        correlate_kernel,
        out_shape=jax.ShapeDtypeStruct((groups, blocks * per_group, block), jnp.float32),
        grid=(groups,),
        in_specs=[
            pl.BlockSpec((1, blocks * per_group, block), lambda g: (g, 0, 0)),
            pl.BlockSpec((1, 1, tokens + block), lambda g: (g, 0, 0)),
        ],
        out_specs=pl.BlockSpec((1, blocks * per_group, block), lambda g: (g, 0, 0)),
        cost_estimate=pl.CostEstimate(
            flops=flops, bytes_accessed=grads.size * 6 + padded.size * 4, transcendentals=0
        ),
    )(shaped, padded)
    out = out.reshape(groups, blocks, per_group, block).transpose(1, 3, 0, 2)
    return out.reshape(tokens, channels)


def on_device(grad_out, qkv_saved, conv_saved, long_taps, short_taps):
    block_rows = grad_out.shape[0]
    out_wide = grad_out.astype(jnp.float32)
    query = qkv_saved[:, 0, :]
    key_part = qkv_saved[:, 1, :]
    value_part = qkv_saved[:, 2, :]
    grad_query = out_wide * conv_saved.astype(jnp.float32)
    grad_mixed = (out_wide * query.astype(jnp.float32)).astype(jnp.bfloat16)
    mixed_cols = lax.all_to_all(grad_mixed, "seq", split_axis=1, concat_axis=0, tiled=True)
    taps_cols = lax.all_to_all(long_taps, "seq", split_axis=1, concat_axis=0, tiled=True)
    short_len = short_taps.shape[1]
    query_proj = short_filter(grad_query[:, None], short_taps[:1], block_rows)
    query_rows = spread_rows(query_proj, "chan")
    z_cols = correlate(mixed_cols, taps_cols)
    grad_z = lax.all_to_all(z_cols, "seq", split_axis=0, concat_axis=1, tiled=True)
    grad_key = grad_z * value_part.astype(jnp.float32)
    grad_value = grad_z * key_part.astype(jnp.float32)
    stacked = jnp.stack([grad_key, grad_value], 1)
    pair_proj = short_filter(stacked, short_taps[1:], block_rows)
    pair_rows = spread_rows(pair_proj, "chan")
    return jnp.concatenate([query_rows, pair_rows], 1)


def spread_rows(value, axis):
    count = lax.axis_size(axis)
    me = lax.axis_index(axis)
    rows, planes, channels = value.shape
    chunks = value.reshape(count, rows // count, planes, channels)
    pieces = [lax.dynamic_index_in_dim(chunks, me, 0, keepdims=False)]
    for step in range(1, count):
        outgoing = lax.dynamic_index_in_dim(chunks, (me + step) % count, 0, keepdims=False)
        pairs = [(source, (source + step) % count) for source in range(count)]
        pieces.append(lax.ppermute(outgoing, axis, pairs))
    gathered = jnp.stack(pieces)
    order = (me - jnp.arange(count)) % count
    placed = jnp.take(gathered, order, axis=0)
    return placed.transpose(1, 2, 0, 3).reshape(rows // count, planes, count * channels)


def short_filter(stacked, taps, block_rows):
    short_len = taps.shape[1]
    borrowed = shifted(stacked[: short_len - 1], "seq", -1)
    extended = jnp.concatenate([stacked, borrowed], 0)
    result = jnp.zeros_like(stacked)
    for lag_index in range(short_len):
        result = result + taps[:, lag_index, :][None] * extended[lag_index : lag_index + block_rows]
    return result.astype(jnp.bfloat16)


def solution(mesh):
    in_specs = (
        P("seq", "chan"),
        P("seq", None, "chan"),
        P("seq", "chan"),
        P("seq", "chan"),
        P(None, None, "chan"),
    )
    out_specs = P(("seq", "chan"), None, None)
    return jax.shard_map(
        on_device, mesh=mesh, in_specs=in_specs, out_specs=out_specs, check_vma=False
    )
```

```python
import functools

import jax
import jax.numpy as jnp
from jax import lax
from jax.experimental import pallas as pl
from jax.experimental.pallas import tpu as pltpu
from jax.sharding import PartitionSpec as P

block = 256
per_group = 16


def shifted(value, axis, steps):
    count = lax.axis_size(axis)
    leading, last = (max(0, -steps), min(count, count - steps))
    return lax.ppermute(value, axis, [(source, source + steps) for source in range(leading, last)])


def correlate_kernel(x_ref, h_ref, o_ref):
    rows_all = x_ref.shape[1]
    blocks = rows_all // per_group
    tokens = blocks * block
    o_ref[...] = jnp.zeros(o_ref.shape, o_ref.dtype)
    for lag_block in range(blocks):
        start = tokens - block * (lag_block + 1)
        window = h_ref[0, :, start : start + 2 * block]
        spread = jnp.broadcast_to(window, (block, 2 * block))
        rolled = pltpu.roll(spread, block + 1, 1, stride=1, stride_axis=0)
        band = rolled[:, :block].astype(jnp.bfloat16)
        rows = per_group * (blocks - lag_block)
        source = x_ref[0, per_group * lag_block :, :]
        o_ref[0, :rows, :] += jnp.dot(source, band, preferred_element_type=jnp.float32)


def correlate(grads, taps):
    tokens, channels = grads.shape
    groups = taps.shape[1]
    blocks = tokens // block
    shaped = grads.reshape(blocks, block, groups, per_group).transpose(2, 0, 3, 1)
    shaped = shaped.reshape(groups, blocks * per_group, block)
    reversed_taps = taps.astype(jnp.float32).T[:, ::-1]
    padded = jnp.concatenate([reversed_taps, jnp.zeros((groups, block), jnp.float32)], 1)
    padded = padded.reshape(groups, 1, tokens + block)
    flops = 2 * groups * per_group * block * block * blocks * (blocks + 1) // 2
    out = pl.pallas_call(
        correlate_kernel,
        out_shape=jax.ShapeDtypeStruct((groups, blocks * per_group, block), jnp.float32),
        grid=(groups,),
        in_specs=[
            pl.BlockSpec((1, blocks * per_group, block), lambda g: (g, 0, 0)),
            pl.BlockSpec((1, 1, tokens + block), lambda g: (g, 0, 0)),
        ],
        out_specs=pl.BlockSpec((1, blocks * per_group, block), lambda g: (g, 0, 0)),
        cost_estimate=pl.CostEstimate(
            flops=flops, bytes_accessed=grads.size * 6 + padded.size * 4, transcendentals=0
        ),
    )(shaped, padded)
    out = out.reshape(groups, blocks, per_group, block).transpose(1, 3, 0, 2)
    return out.reshape(tokens, channels)


def on_device(grad_out, qkv_saved, conv_saved, long_taps, short_taps):
    block_rows = grad_out.shape[0]
    out_wide = grad_out.astype(jnp.float32)
    query = qkv_saved[:, 0, :]
    key_part = qkv_saved[:, 1, :]
    value_part = qkv_saved[:, 2, :]
    grad_query = out_wide * conv_saved.astype(jnp.float32)
    grad_mixed = (out_wide * query.astype(jnp.float32)).astype(jnp.bfloat16)
    mixed_cols = lax.all_to_all(grad_mixed, "seq", split_axis=1, concat_axis=0, tiled=True)
    taps_cols = lax.all_to_all(long_taps, "seq", split_axis=1, concat_axis=0, tiled=True)
    short_len = short_taps.shape[1]
    query_proj = short_filter(grad_query[:, None], short_taps[:1], block_rows)
    query_rows = spread_rows(query_proj, "chan")
    z_cols = correlate(mixed_cols, taps_cols)
    z_cols, query_rows = lax.optimization_barrier((z_cols, query_rows))
    grad_z = lax.all_to_all(z_cols, "seq", split_axis=0, concat_axis=1, tiled=True)
    grad_key = grad_z * value_part.astype(jnp.float32)
    grad_value = grad_z * key_part.astype(jnp.float32)
    stacked = jnp.stack([grad_key, grad_value], 1)
    pair_proj = short_filter(stacked, short_taps[1:], block_rows)
    pair_rows = spread_rows(pair_proj, "chan")
    return jnp.concatenate([query_rows, pair_rows], 1)


def spread_rows(value, axis):
    count = lax.axis_size(axis)
    me = lax.axis_index(axis)
    rows, planes, channels = value.shape
    chunks = value.reshape(count, rows // count, planes, channels)
    pieces = [lax.dynamic_index_in_dim(chunks, me, 0, keepdims=False)]
    for step in range(1, count):
        outgoing = lax.dynamic_index_in_dim(chunks, (me + step) % count, 0, keepdims=False)
        pairs = [(source, (source + step) % count) for source in range(count)]
        pieces.append(lax.ppermute(outgoing, axis, pairs))
    gathered = jnp.stack(pieces)
    order = (me - jnp.arange(count)) % count
    placed = jnp.take(gathered, order, axis=0)
    return placed.transpose(1, 2, 0, 3).reshape(rows // count, planes, count * channels)


def short_filter(stacked, taps, block_rows):
    short_len = taps.shape[1]
    borrowed = shifted(stacked[: short_len - 1], "seq", -1)
    extended = jnp.concatenate([stacked, borrowed], 0)
    result = jnp.zeros_like(stacked)
    for lag_index in range(short_len):
        result = result + taps[:, lag_index, :][None] * extended[lag_index : lag_index + block_rows]
    return result.astype(jnp.bfloat16)


def solution(mesh):
    in_specs = (
        P("seq", "chan"),
        P("seq", None, "chan"),
        P("seq", "chan"),
        P("seq", "chan"),
        P(None, None, "chan"),
    )
    out_specs = P(("seq", "chan"), None, None)
    return jax.shard_map(
        on_device, mesh=mesh, in_specs=in_specs, out_specs=out_specs, check_vma=False
    )
```

```python
import functools

import jax
import jax.numpy as jnp
from jax import lax
from jax.experimental import pallas as pl
from jax.experimental.pallas import tpu as pltpu
from jax.sharding import PartitionSpec as P

block = 256
per_group = 16


def shifted(value, axis, steps):
    count = lax.axis_size(axis)
    leading, last = (max(0, -steps), min(count, count - steps))
    return lax.ppermute(value, axis, [(source, source + steps) for source in range(leading, last)])


def correlate_kernel(x_ref, h_ref, o_ref):
    rows_all = x_ref.shape[1]
    blocks = rows_all // per_group
    tokens = blocks * block
    o_ref[...] = jnp.zeros(o_ref.shape, o_ref.dtype)
    for lag_block in range(blocks):
        start = tokens - block * (lag_block + 1)
        window = h_ref[0, :, start : start + 2 * block]
        spread = jnp.broadcast_to(window, (block, 2 * block))
        rolled = pltpu.roll(spread, block + 1, 1, stride=1, stride_axis=0)
        band = rolled[:, :block].astype(jnp.bfloat16)
        rows = per_group * (blocks - lag_block)
        source = x_ref[0, per_group * lag_block :, :]
        o_ref[0, :rows, :] += jnp.dot(source, band, preferred_element_type=jnp.float32)


def correlate(grads, taps):
    tokens, channels = grads.shape
    groups = taps.shape[1]
    blocks = tokens // block
    shaped = grads.reshape(blocks, block, groups, per_group).transpose(2, 0, 3, 1)
    shaped = shaped.reshape(groups, blocks * per_group, block)
    reversed_taps = taps.astype(jnp.float32).T[:, ::-1]
    padded = jnp.concatenate([reversed_taps, jnp.zeros((groups, block), jnp.float32)], 1)
    padded = padded.reshape(groups, 1, tokens + block)
    flops = 2 * groups * per_group * block * block * blocks * (blocks + 1) // 2
    out = pl.pallas_call(
        correlate_kernel,
        out_shape=jax.ShapeDtypeStruct((groups, blocks * per_group, block), jnp.float32),
        grid=(groups,),
        in_specs=[
            pl.BlockSpec((1, blocks * per_group, block), lambda g: (g, 0, 0)),
            pl.BlockSpec((1, 1, tokens + block), lambda g: (g, 0, 0)),
        ],
        out_specs=pl.BlockSpec((1, blocks * per_group, block), lambda g: (g, 0, 0)),
        cost_estimate=pl.CostEstimate(
            flops=flops, bytes_accessed=grads.size * 6 + padded.size * 4, transcendentals=0
        ),
    )(shaped, padded)
    out = out.reshape(groups, blocks, per_group, block).transpose(1, 3, 0, 2)
    return out.reshape(tokens, channels)


def on_device(grad_out, qkv_saved, conv_saved, long_taps, short_taps):
    block_rows = grad_out.shape[0]
    out_wide = grad_out.astype(jnp.float32)
    query = qkv_saved[:, 0, :]
    key_part = qkv_saved[:, 1, :]
    value_part = qkv_saved[:, 2, :]
    grad_query = out_wide * conv_saved.astype(jnp.float32)
    grad_mixed = (out_wide * query.astype(jnp.float32)).astype(jnp.bfloat16)
    mixed_cols = lax.all_to_all(grad_mixed, "seq", split_axis=1, concat_axis=0, tiled=True)
    taps_cols = lax.all_to_all(long_taps, "seq", split_axis=1, concat_axis=0, tiled=True)
    short_len = short_taps.shape[1]
    query_proj = short_filter(grad_query[:, None], short_taps[:1], block_rows)
    query_rows = spread_rows(query_proj, "chan")
    z_cols = correlate(mixed_cols, taps_cols)
    z_narrow = z_cols.astype(jnp.bfloat16)
    grad_z = lax.all_to_all(z_narrow, "seq", split_axis=0, concat_axis=1, tiled=True)
    grad_z = grad_z.astype(jnp.float32)
    grad_key = grad_z * value_part.astype(jnp.float32)
    grad_value = grad_z * key_part.astype(jnp.float32)
    stacked = jnp.stack([grad_key, grad_value], 1)
    pair_proj = short_filter(stacked, short_taps[1:], block_rows)
    pair_rows = spread_rows(pair_proj, "chan")
    return jnp.concatenate([query_rows, pair_rows], 1)


def spread_rows(value, axis):
    count = lax.axis_size(axis)
    me = lax.axis_index(axis)
    rows, planes, channels = value.shape
    chunks = value.reshape(count, rows // count, planes, channels)
    pieces = [lax.dynamic_index_in_dim(chunks, me, 0, keepdims=False)]
    for step in range(1, count):
        outgoing = lax.dynamic_index_in_dim(chunks, (me + step) % count, 0, keepdims=False)
        pairs = [(source, (source + step) % count) for source in range(count)]
        pieces.append(lax.ppermute(outgoing, axis, pairs))
    gathered = jnp.stack(pieces)
    order = (me - jnp.arange(count)) % count
    placed = jnp.take(gathered, order, axis=0)
    return placed.transpose(1, 2, 0, 3).reshape(rows // count, planes, count * channels)


def short_filter(stacked, taps, block_rows):
    short_len = taps.shape[1]
    borrowed = shifted(stacked[: short_len - 1], "seq", -1)
    extended = jnp.concatenate([stacked, borrowed], 0)
    result = jnp.zeros_like(stacked)
    for lag_index in range(short_len):
        result = result + taps[:, lag_index, :][None] * extended[lag_index : lag_index + block_rows]
    return result.astype(jnp.bfloat16)


def solution(mesh):
    in_specs = (
        P("seq", "chan"),
        P("seq", None, "chan"),
        P("seq", "chan"),
        P("seq", "chan"),
        P(None, None, "chan"),
    )
    out_specs = P(("seq", "chan"), None, None)
    return jax.shard_map(
        on_device, mesh=mesh, in_specs=in_specs, out_specs=out_specs, check_vma=False
    )
```

```python
import functools

import jax
import jax.numpy as jnp
from jax import lax
from jax.experimental import pallas as pl
from jax.experimental.pallas import tpu as pltpu
from jax.sharding import PartitionSpec as P

block = 256
per_group = 16


def shifted(value, axis, steps):
    count = lax.axis_size(axis)
    leading, last = (max(0, -steps), min(count, count - steps))
    return lax.ppermute(value, axis, [(source, source + steps) for source in range(leading, last)])


def correlate_kernel(x_ref, h_ref, o_ref):
    rows_all = x_ref.shape[1]
    blocks = rows_all // per_group
    tokens = blocks * block
    o_ref[...] = jnp.zeros(o_ref.shape, o_ref.dtype)
    for lag_block in range(blocks):
        start = tokens - block * (lag_block + 1)
        window = h_ref[0, :, start : start + 2 * block]
        spread = jnp.broadcast_to(window, (block, 2 * block))
        rolled = pltpu.roll(spread, block + 1, 1, stride=1, stride_axis=0)
        band = rolled[:, :block].astype(jnp.bfloat16)
        rows = per_group * (blocks - lag_block)
        source = x_ref[0, per_group * lag_block :, :]
        o_ref[0, :rows, :] += jnp.dot(source, band, preferred_element_type=jnp.float32)


def correlate(grads, taps):
    tokens, channels = grads.shape
    groups = taps.shape[1]
    blocks = tokens // block
    shaped = grads.reshape(blocks, block, groups, per_group).transpose(2, 0, 3, 1)
    shaped = shaped.reshape(groups, blocks * per_group, block)
    reversed_taps = taps.astype(jnp.float32).T[:, ::-1]
    padded = jnp.concatenate([reversed_taps, jnp.zeros((groups, block), jnp.float32)], 1)
    padded = padded.reshape(groups, 1, tokens + block)
    flops = 2 * groups * per_group * block * block * blocks * (blocks + 1) // 2
    out = pl.pallas_call(
        correlate_kernel,
        out_shape=jax.ShapeDtypeStruct((groups, blocks * per_group, block), jnp.float32),
        grid=(groups,),
        in_specs=[
            pl.BlockSpec((1, blocks * per_group, block), lambda g: (g, 0, 0)),
            pl.BlockSpec((1, 1, tokens + block), lambda g: (g, 0, 0)),
        ],
        out_specs=pl.BlockSpec((1, blocks * per_group, block), lambda g: (g, 0, 0)),
        cost_estimate=pl.CostEstimate(
            flops=flops, bytes_accessed=grads.size * 6 + padded.size * 4, transcendentals=0
        ),
    )(shaped, padded)
    out = out.reshape(groups, blocks, per_group, block).transpose(1, 3, 0, 2)
    return out.reshape(tokens, channels)


def on_device(grad_out, qkv_saved, conv_saved, long_taps, short_taps):
    block_rows = grad_out.shape[0]
    out_wide = grad_out.astype(jnp.float32)
    query = qkv_saved[:, 0, :]
    key_part = qkv_saved[:, 1, :]
    value_part = qkv_saved[:, 2, :]
    grad_query = out_wide * conv_saved.astype(jnp.float32)
    grad_mixed = (out_wide * query.astype(jnp.float32)).astype(jnp.bfloat16)
    mixed_cols = lax.all_to_all(grad_mixed, "seq", split_axis=1, concat_axis=0, tiled=True)
    taps_cols = lax.all_to_all(long_taps, "seq", split_axis=1, concat_axis=0, tiled=True)
    short_len = short_taps.shape[1]
    query_proj = short_filter(grad_query[:, None], short_taps[:1], block_rows)
    query_rows = spread_rows(query_proj, "chan")
    z_cols = correlate(mixed_cols, taps_cols)
    z_narrow = z_cols.astype(jnp.bfloat16)
    grad_z = lax.all_to_all(z_narrow, "seq", split_axis=0, concat_axis=1, tiled=True)
    grad_z = grad_z.astype(jnp.float32)
    grad_key = grad_z * value_part.astype(jnp.float32)
    grad_value = grad_z * key_part.astype(jnp.float32)
    stacked = jnp.stack([grad_key, grad_value], 1)
    pair_proj = short_filter(stacked, short_taps[1:], block_rows)
    pair_rows = spread_rows(pair_proj, "chan")
    count = lax.axis_size("chan")
    return place_rows([query_rows, pair_rows], count, block_rows // count, grad_out.shape[1])


def spread_rows(value, axis):
    count = lax.axis_size(axis)
    me = lax.axis_index(axis)
    rows, planes, channels = value.shape
    chunks = value.reshape(count, rows // count, planes, channels)
    pieces = [(me, lax.dynamic_index_in_dim(chunks, me, 0, keepdims=False))]
    for step in range(1, count):
        outgoing = lax.dynamic_index_in_dim(chunks, (me + step) % count, 0, keepdims=False)
        pairs = [(source, (source + step) % count) for source in range(count)]
        pieces.append(((me + count - step) % count, lax.ppermute(outgoing, axis, pairs)))
    return pieces


def place_rows(parts, count, rows, channels):
    planes = sum(pieces[0][1].shape[1] for pieces in parts)
    out = jnp.zeros((rows, planes, count * channels), parts[0][0][1].dtype)
    plane = 0
    for pieces in parts:
        for source, piece in pieces:
            out = lax.dynamic_update_slice(out, piece, (0, plane, source * channels))
        plane += pieces[0][1].shape[1]
    return out


def short_filter(stacked, taps, block_rows):
    short_len = taps.shape[1]
    borrowed = shifted(stacked[: short_len - 1], "seq", -1)
    extended = jnp.concatenate([stacked, borrowed], 0)
    result = jnp.zeros_like(stacked)
    for lag_index in range(short_len):
        result = result + taps[:, lag_index, :][None] * extended[lag_index : lag_index + block_rows]
    return result.astype(jnp.bfloat16)


def solution(mesh):
    in_specs = (
        P("seq", "chan"),
        P("seq", None, "chan"),
        P("seq", "chan"),
        P("seq", "chan"),
        P(None, None, "chan"),
    )
    out_specs = P(("seq", "chan"), None, None)
    return jax.shard_map(
        on_device, mesh=mesh, in_specs=in_specs, out_specs=out_specs, check_vma=False
    )
```

```python
import functools

import jax
import jax.numpy as jnp
from jax import lax
from jax.experimental import pallas as pl
from jax.experimental.pallas import tpu as pltpu
from jax.sharding import PartitionSpec as P

block = 256
per_group = 16


def shifted(value, axis, steps):
    count = lax.axis_size(axis)
    leading, last = (max(0, -steps), min(count, count - steps))
    return lax.ppermute(value, axis, [(source, source + steps) for source in range(leading, last)])


def correlate_kernel(x_ref, h_ref, o_ref):
    rows_all = x_ref.shape[1]
    blocks = rows_all // per_group
    tokens = blocks * block
    o_ref[...] = jnp.zeros(o_ref.shape, o_ref.dtype)
    for lag_block in range(blocks):
        start = tokens - block * (lag_block + 1)
        window = h_ref[0, :, start : start + 2 * block]
        spread = jnp.broadcast_to(window, (block, 2 * block))
        rolled = pltpu.roll(spread, block + 1, 1, stride=1, stride_axis=0)
        band = rolled[:, :block].astype(jnp.bfloat16)
        rows = per_group * (blocks - lag_block)
        source = x_ref[0, per_group * lag_block :, :]
        o_ref[0, :rows, :] += jnp.dot(source, band, preferred_element_type=jnp.float32)


def correlate(grads, taps):
    tokens, channels = grads.shape
    groups = taps.shape[1]
    blocks = tokens // block
    shaped = grads.reshape(blocks, block, groups, per_group).transpose(2, 0, 3, 1)
    shaped = shaped.reshape(groups, blocks * per_group, block)
    reversed_taps = taps.astype(jnp.float32).T[:, ::-1]
    padded = jnp.concatenate([reversed_taps, jnp.zeros((groups, block), jnp.float32)], 1)
    padded = padded.reshape(groups, 1, tokens + block)
    flops = 2 * groups * per_group * block * block * blocks * (blocks + 1) // 2
    out = pl.pallas_call(
        correlate_kernel,
        out_shape=jax.ShapeDtypeStruct((groups, blocks * per_group, block), jnp.float32),
        grid=(groups,),
        in_specs=[
            pl.BlockSpec((1, blocks * per_group, block), lambda g: (g, 0, 0)),
            pl.BlockSpec((1, 1, tokens + block), lambda g: (g, 0, 0)),
        ],
        out_specs=pl.BlockSpec((1, blocks * per_group, block), lambda g: (g, 0, 0)),
        cost_estimate=pl.CostEstimate(
            flops=flops, bytes_accessed=grads.size * 6 + padded.size * 4, transcendentals=0
        ),
    )(shaped, padded)
    out = out.reshape(groups, blocks, per_group, block).transpose(1, 3, 0, 2)
    return out.reshape(tokens, channels)


def on_device(grad_out, qkv_saved, conv_saved, long_taps, short_taps):
    block_rows, channels = grad_out.shape
    out_wide = grad_out.astype(jnp.float32)
    query = qkv_saved[:, 0, :]
    key_part = qkv_saved[:, 1, :]
    value_part = qkv_saved[:, 2, :]
    grad_query = out_wide * conv_saved.astype(jnp.float32)
    grad_mixed = (out_wide * query.astype(jnp.float32)).astype(jnp.bfloat16)
    mixed_cols = lax.all_to_all(grad_mixed, "seq", split_axis=1, concat_axis=0, tiled=True)
    taps_cols = lax.all_to_all(long_taps, "seq", split_axis=1, concat_axis=0, tiled=True)
    query_rows = spread_rows(short_filter(grad_query, short_taps[0]), "chan")
    z_cols = correlate(mixed_cols, taps_cols)
    shards = lax.axis_size("seq")
    z_narrow = z_cols.astype(jnp.bfloat16).reshape(shards, block_rows, -1)
    z_split = lax.all_to_all(z_narrow, "seq", split_axis=0, concat_axis=0, tiled=True)
    z_split = z_split.astype(jnp.float32)
    width = z_split.shape[2]
    value_split = value_part.reshape(block_rows, shards, width).transpose(1, 0, 2)
    key_split = key_part.reshape(block_rows, shards, width).transpose(1, 0, 2)
    grad_key = z_split * value_split.astype(jnp.float32)
    grad_value = z_split * key_split.astype(jnp.float32)
    key_rows = spread_split(split_filter(grad_key, short_taps[1]), "chan")
    value_rows = spread_split(split_filter(grad_value, short_taps[2]), "chan")
    count = lax.axis_size("chan")
    planes = [query_rows, key_rows, value_rows]
    out = jnp.zeros((block_rows // count, len(planes), count * channels), jnp.bfloat16)
    for plane, pieces in enumerate(planes):
        for source, piece in pieces:
            out = lax.dynamic_update_slice(out, piece[:, None, :], (0, plane, source * channels))
    return out


def spread_rows(value, axis):
    count = lax.axis_size(axis)
    me = lax.axis_index(axis)
    rows, channels = value.shape
    chunks = value.reshape(count, rows // count, channels)
    pieces = [(me, lax.dynamic_index_in_dim(chunks, me, 0, keepdims=False))]
    for step in range(1, count):
        outgoing = lax.dynamic_index_in_dim(chunks, (me + step) % count, 0, keepdims=False)
        pairs = [(source, (source + step) % count) for source in range(count)]
        pieces.append(((me + count - step) % count, lax.ppermute(outgoing, axis, pairs)))
    return pieces


def split_filter(rows, taps):
    shards, block_rows, width = rows.shape
    short_len = taps.shape[0]
    taps = taps.reshape(short_len, shards, 1, width)
    borrowed = shifted(rows[:, : short_len - 1], "seq", -1)
    extended = jnp.concatenate([rows, borrowed], 1)
    result = jnp.zeros_like(rows)
    for lag_index in range(short_len):
        result = result + taps[lag_index] * extended[:, lag_index : lag_index + block_rows]
    return result.astype(jnp.bfloat16)


def spread_split(value, axis):
    count = lax.axis_size(axis)
    me = lax.axis_index(axis)
    shards, rows, width = value.shape
    chunks = value.reshape(shards, count, rows // count, width)

    def flat(piece):
        return piece.transpose(1, 0, 2).reshape(rows // count, shards * width)

    pieces = [(me, flat(lax.dynamic_index_in_dim(chunks, me, 1, keepdims=False)))]
    for step in range(1, count):
        outgoing = lax.dynamic_index_in_dim(chunks, (me + step) % count, 1, keepdims=False)
        pairs = [(source, (source + step) % count) for source in range(count)]
        pieces.append(((me + count - step) % count, flat(lax.ppermute(outgoing, axis, pairs))))
    return pieces


def short_filter(rows, taps):
    block_rows = rows.shape[0]
    short_len = taps.shape[0]
    borrowed = shifted(rows[: short_len - 1], "seq", -1)
    extended = jnp.concatenate([rows, borrowed], 0)
    result = jnp.zeros_like(rows)
    for lag_index in range(short_len):
        result = result + taps[lag_index][None] * extended[lag_index : lag_index + block_rows]
    return result.astype(jnp.bfloat16)


def solution(mesh):
    in_specs = (
        P("seq", "chan"),
        P("seq", None, "chan"),
        P("seq", "chan"),
        P("seq", "chan"),
        P(None, None, "chan"),
    )
    out_specs = P(("seq", "chan"), None, None)
    return jax.shard_map(
        on_device, mesh=mesh, in_specs=in_specs, out_specs=out_specs, check_vma=False
    )
```

```python
import functools

import jax
import jax.numpy as jnp
from jax import lax
from jax.experimental import pallas as pl
from jax.experimental.pallas import tpu as pltpu
from jax.sharding import PartitionSpec as P

block = 256
per_group = 16


def shifted(value, axis, steps):
    count = lax.axis_size(axis)
    leading, last = (max(0, -steps), min(count, count - steps))
    return lax.ppermute(value, axis, [(source, source + steps) for source in range(leading, last)])


def correlate_kernel(x_ref, h_ref, o_ref, acc_ref):
    rows_all = x_ref.shape[1]
    blocks = rows_all // per_group
    tokens = blocks * block
    acc_ref[...] = jnp.zeros(acc_ref.shape, acc_ref.dtype)
    for lag_block in range(blocks):
        start = tokens - block * (lag_block + 1)
        window = h_ref[0, :, start : start + 2 * block]
        spread = jnp.broadcast_to(window, (block, 2 * block))
        rolled = pltpu.roll(spread, block + 1, 1, stride=1, stride_axis=0)
        band = rolled[:, :block].astype(jnp.bfloat16)
        rows = per_group * (blocks - lag_block)
        source = x_ref[0, per_group * lag_block :, :]
        acc_ref[:rows, :] += jnp.dot(source, band, preferred_element_type=jnp.float32)
    for index in range(blocks):
        slab = acc_ref[per_group * index : per_group * (index + 1), :]
        o_ref[:, block * index : block * (index + 1)] = slab.astype(o_ref.dtype)


def correlate(grads, taps):
    tokens, channels = grads.shape
    groups = taps.shape[1]
    blocks = tokens // block
    shaped = grads.reshape(blocks, block, groups, per_group).transpose(2, 0, 3, 1)
    shaped = shaped.reshape(groups, blocks * per_group, block)
    reversed_taps = taps.astype(jnp.float32).T[:, ::-1]
    padded = jnp.concatenate([reversed_taps, jnp.zeros((groups, block), jnp.float32)], 1)
    padded = padded.reshape(groups, 1, tokens + block)
    flops = 2 * groups * per_group * block * block * blocks * (blocks + 1) // 2
    return pl.pallas_call(
        correlate_kernel,
        out_shape=jax.ShapeDtypeStruct((channels, tokens), jnp.bfloat16),
        grid=(groups,),
        in_specs=[
            pl.BlockSpec((1, blocks * per_group, block), lambda g: (g, 0, 0)),
            pl.BlockSpec((1, 1, tokens + block), lambda g: (g, 0, 0)),
        ],
        out_specs=pl.BlockSpec((per_group, tokens), lambda g: (g, 0)),
        scratch_shapes=[pltpu.VMEM((blocks * per_group, block), jnp.float32)],
        cost_estimate=pl.CostEstimate(
            flops=flops, bytes_accessed=grads.size * 4 + padded.size * 4, transcendentals=0
        ),
    )(shaped, padded)


def on_device(grad_out, qkv_saved, conv_saved, long_taps, short_taps):
    block_rows, channels = grad_out.shape
    out_wide = grad_out.astype(jnp.float32)
    query = qkv_saved[:, 0, :]
    key_part = qkv_saved[:, 1, :]
    value_part = qkv_saved[:, 2, :]
    grad_query = out_wide * conv_saved.astype(jnp.float32)
    grad_mixed = (out_wide * query.astype(jnp.float32)).astype(jnp.bfloat16)
    mixed_cols = lax.all_to_all(grad_mixed, "seq", split_axis=1, concat_axis=0, tiled=True)
    taps_cols = lax.all_to_all(long_taps, "seq", split_axis=1, concat_axis=0, tiled=True)
    short_len = short_taps.shape[1]
    query_proj = short_filter(grad_query[:, None], short_taps[:1], block_rows)
    query_rows = spread_rows(query_proj, "chan")
    z_lanes = correlate(mixed_cols, taps_cols)
    z_rows = lax.all_to_all(z_lanes, "seq", split_axis=1, concat_axis=0, tiled=True)
    z_wide = z_rows.astype(jnp.float32)
    grad_key = z_wide * value_part.T.astype(jnp.float32)
    grad_value = z_wide * key_part.T.astype(jnp.float32)
    count = lax.axis_size("chan")
    out = jnp.zeros((block_rows // count, 3, count * channels), jnp.bfloat16)
    for source, piece in query_rows:
        out = lax.dynamic_update_slice(out, piece, (0, 0, source * channels))
    for plane, lanes in ((1, grad_key), (2, grad_value)):
        filtered = lane_filter(lanes, short_taps[plane])
        for source, piece in spread_lanes(filtered, "chan"):
            out = lax.dynamic_update_slice(out, piece.T[:, None, :], (0, plane, source * channels))
    return out


def lane_filter(lanes, taps):
    block_rows = lanes.shape[1]
    short_len = taps.shape[0]
    borrowed = shifted(lanes[:, : short_len - 1], "seq", -1)
    extended = jnp.concatenate([lanes, borrowed], 1)
    result = jnp.zeros_like(lanes)
    for lag_index in range(short_len):
        result = result + taps[lag_index][:, None] * extended[:, lag_index : lag_index + block_rows]
    return result.astype(jnp.bfloat16)


def spread_lanes(value, axis):
    count = lax.axis_size(axis)
    me = lax.axis_index(axis)
    width = value.shape[1] // count

    def lanes_for(index):
        return lax.dynamic_slice_in_dim(value, pl.multiple_of(index * width, width), width, 1)

    pieces = [(me, lanes_for(me))]
    for step in range(1, count):
        pairs = [(source, (source + step) % count) for source in range(count)]
        outgoing = lanes_for((me + step) % count)
        pieces.append(((me + count - step) % count, lax.ppermute(outgoing, axis, pairs)))
    return pieces


def spread_rows(value, axis):
    count = lax.axis_size(axis)
    me = lax.axis_index(axis)
    rows, planes, channels = value.shape
    chunks = value.reshape(count, rows // count, planes, channels)
    pieces = [(me, lax.dynamic_index_in_dim(chunks, me, 0, keepdims=False))]
    for step in range(1, count):
        outgoing = lax.dynamic_index_in_dim(chunks, (me + step) % count, 0, keepdims=False)
        pairs = [(source, (source + step) % count) for source in range(count)]
        pieces.append(((me + count - step) % count, lax.ppermute(outgoing, axis, pairs)))
    return pieces


def place_rows(parts, count, rows, channels):
    planes = sum(pieces[0][1].shape[1] for pieces in parts)
    out = jnp.zeros((rows, planes, count * channels), parts[0][0][1].dtype)
    plane = 0
    for pieces in parts:
        for source, piece in pieces:
            out = lax.dynamic_update_slice(out, piece, (0, plane, source * channels))
        plane += pieces[0][1].shape[1]
    return out


def short_filter(stacked, taps, block_rows):
    short_len = taps.shape[1]
    borrowed = shifted(stacked[: short_len - 1], "seq", -1)
    extended = jnp.concatenate([stacked, borrowed], 0)
    result = jnp.zeros_like(stacked)
    for lag_index in range(short_len):
        result = result + taps[:, lag_index, :][None] * extended[lag_index : lag_index + block_rows]
    return result.astype(jnp.bfloat16)


def solution(mesh):
    in_specs = (
        P("seq", "chan"),
        P("seq", None, "chan"),
        P("seq", "chan"),
        P("seq", "chan"),
        P(None, None, "chan"),
    )
    out_specs = P(("seq", "chan"), None, None)
    return jax.shard_map(
        on_device, mesh=mesh, in_specs=in_specs, out_specs=out_specs, check_vma=False
    )
```

```python
import functools

import jax
import jax.numpy as jnp
from jax import lax
from jax.experimental import pallas as pl
from jax.experimental.pallas import tpu as pltpu
from jax.sharding import PartitionSpec as P

block = 256
per_group = 16


def shifted(value, axis, steps):
    count = lax.axis_size(axis)
    leading, last = (max(0, -steps), min(count, count - steps))
    return lax.ppermute(value, axis, [(source, source + steps) for source in range(leading, last)])


def correlate_kernel(x_ref, h_ref, o_ref, acc_ref):
    rows_all = x_ref.shape[1]
    blocks = rows_all // per_group
    tokens = blocks * block
    acc_ref[...] = jnp.zeros(acc_ref.shape, acc_ref.dtype)
    for lag_block in range(blocks):
        start = tokens - block * (lag_block + 1)
        window = h_ref[0, :, start : start + 2 * block]
        spread = jnp.broadcast_to(window, (block, 2 * block))
        rolled = pltpu.roll(spread, block + 1, 1, stride=1, stride_axis=0)
        band = rolled[:, :block].astype(jnp.bfloat16)
        rows = per_group * (blocks - lag_block)
        source = x_ref[0, per_group * lag_block :, :]
        acc_ref[:rows, :] += jnp.dot(source, band, preferred_element_type=jnp.float32)
    for index in range(blocks):
        slab = acc_ref[per_group * index : per_group * (index + 1), :]
        o_ref[:, block * index : block * (index + 1)] = slab.astype(o_ref.dtype)


def correlate(grads, taps):
    tokens, channels = grads.shape
    groups = taps.shape[1]
    blocks = tokens // block
    shaped = grads.reshape(blocks, block, groups, per_group).transpose(2, 0, 3, 1)
    shaped = shaped.reshape(groups, blocks * per_group, block)
    reversed_taps = taps.astype(jnp.float32).T[:, ::-1]
    padded = jnp.concatenate([reversed_taps, jnp.zeros((groups, block), jnp.float32)], 1)
    padded = padded.reshape(groups, 1, tokens + block)
    flops = 2 * groups * per_group * block * block * blocks * (blocks + 1) // 2
    return pl.pallas_call(
        correlate_kernel,
        out_shape=jax.ShapeDtypeStruct((channels, tokens), jnp.bfloat16),
        grid=(groups,),
        in_specs=[
            pl.BlockSpec((1, blocks * per_group, block), lambda g: (g, 0, 0)),
            pl.BlockSpec((1, 1, tokens + block), lambda g: (g, 0, 0)),
        ],
        out_specs=pl.BlockSpec((per_group, tokens), lambda g: (g, 0)),
        scratch_shapes=[pltpu.VMEM((blocks * per_group, block), jnp.float32)],
        cost_estimate=pl.CostEstimate(
            flops=flops, bytes_accessed=grads.size * 4 + padded.size * 4, transcendentals=0
        ),
    )(shaped, padded)


def on_device(grad_out, qkv_saved, conv_saved, long_taps, short_taps):
    block_rows, channels = grad_out.shape
    out_wide = grad_out.astype(jnp.float32)
    query = qkv_saved[:, 0, :]
    key_part = qkv_saved[:, 1, :]
    value_part = qkv_saved[:, 2, :]
    grad_query = out_wide * conv_saved.astype(jnp.float32)
    grad_mixed = (out_wide * query.astype(jnp.float32)).astype(jnp.bfloat16)
    mixed_cols = lax.all_to_all(grad_mixed, "seq", split_axis=1, concat_axis=0, tiled=True)
    taps_cols = lax.all_to_all(long_taps, "seq", split_axis=1, concat_axis=0, tiled=True)
    short_len = short_taps.shape[1]
    query_proj = short_filter(grad_query[:, None], short_taps[:1], block_rows)
    query_rows = spread_rows(query_proj, "chan")
    z_lanes = correlate(mixed_cols, taps_cols)
    z_lanes, query_rows = lax.optimization_barrier((z_lanes, query_rows))
    z_rows = lax.all_to_all(z_lanes, "seq", split_axis=1, concat_axis=0, tiled=True)
    z_wide = z_rows.astype(jnp.float32)
    grad_key = z_wide * value_part.T.astype(jnp.float32)
    grad_value = z_wide * key_part.T.astype(jnp.float32)
    count = lax.axis_size("chan")
    out = jnp.zeros((block_rows // count, 3, count * channels), jnp.bfloat16)
    for source, piece in query_rows:
        out = lax.dynamic_update_slice(out, piece, (0, 0, source * channels))
    for plane, lanes in ((1, grad_key), (2, grad_value)):
        filtered = lane_filter(lanes, short_taps[plane])
        for source, piece in spread_lanes(filtered, "chan"):
            out = lax.dynamic_update_slice(out, piece.T[:, None, :], (0, plane, source * channels))
    return out


def lane_filter(lanes, taps):
    block_rows = lanes.shape[1]
    short_len = taps.shape[0]
    borrowed = shifted(lanes[:, : short_len - 1], "seq", -1)
    extended = jnp.concatenate([lanes, borrowed], 1)
    result = jnp.zeros_like(lanes)
    for lag_index in range(short_len):
        result = result + taps[lag_index][:, None] * extended[:, lag_index : lag_index + block_rows]
    return result.astype(jnp.bfloat16)


def spread_lanes(value, axis):
    count = lax.axis_size(axis)
    me = lax.axis_index(axis)
    width = value.shape[1] // count

    def lanes_for(index):
        return lax.dynamic_slice_in_dim(value, pl.multiple_of(index * width, width), width, 1)

    pieces = [(me, lanes_for(me))]
    for step in range(1, count):
        pairs = [(source, (source + step) % count) for source in range(count)]
        outgoing = lanes_for((me + step) % count)
        pieces.append(((me + count - step) % count, lax.ppermute(outgoing, axis, pairs)))
    return pieces


def spread_rows(value, axis):
    count = lax.axis_size(axis)
    me = lax.axis_index(axis)
    rows, planes, channels = value.shape
    chunks = value.reshape(count, rows // count, planes, channels)
    pieces = [(me, lax.dynamic_index_in_dim(chunks, me, 0, keepdims=False))]
    for step in range(1, count):
        outgoing = lax.dynamic_index_in_dim(chunks, (me + step) % count, 0, keepdims=False)
        pairs = [(source, (source + step) % count) for source in range(count)]
        pieces.append(((me + count - step) % count, lax.ppermute(outgoing, axis, pairs)))
    return pieces


def place_rows(parts, count, rows, channels):
    planes = sum(pieces[0][1].shape[1] for pieces in parts)
    out = jnp.zeros((rows, planes, count * channels), parts[0][0][1].dtype)
    plane = 0
    for pieces in parts:
        for source, piece in pieces:
            out = lax.dynamic_update_slice(out, piece, (0, plane, source * channels))
        plane += pieces[0][1].shape[1]
    return out


def short_filter(stacked, taps, block_rows):
    short_len = taps.shape[1]
    borrowed = shifted(stacked[: short_len - 1], "seq", -1)
    extended = jnp.concatenate([stacked, borrowed], 0)
    result = jnp.zeros_like(stacked)
    for lag_index in range(short_len):
        result = result + taps[:, lag_index, :][None] * extended[lag_index : lag_index + block_rows]
    return result.astype(jnp.bfloat16)


def solution(mesh):
    in_specs = (
        P("seq", "chan"),
        P("seq", None, "chan"),
        P("seq", "chan"),
        P("seq", "chan"),
        P(None, None, "chan"),
    )
    out_specs = P(("seq", "chan"), None, None)
    return jax.shard_map(
        on_device, mesh=mesh, in_specs=in_specs, out_specs=out_specs, check_vma=False
    )
```

```python
import functools

import jax
import jax.numpy as jnp
from jax import lax
from jax.experimental import pallas as pl
from jax.experimental.pallas import tpu as pltpu
from jax.sharding import PartitionSpec as P

block = 256
per_group = 16


def shifted(value, axis, steps):
    count = lax.axis_size(axis)
    leading, last = (max(0, -steps), min(count, count - steps))
    return lax.ppermute(value, axis, [(source, source + steps) for source in range(leading, last)])


def correlate_kernel(x_ref, h_ref, o_ref, acc_ref):
    rows_all = x_ref.shape[1]
    blocks = rows_all // per_group
    tokens = blocks * block
    acc_ref[...] = jnp.zeros(acc_ref.shape, acc_ref.dtype)
    for lag_block in range(blocks):
        start = tokens - block * (lag_block + 1)
        window = h_ref[0, :, start : start + 2 * block]
        spread = jnp.broadcast_to(window, (block, 2 * block))
        rolled = pltpu.roll(spread, block + 1, 1, stride=1, stride_axis=0)
        band = rolled[:, :block].astype(jnp.bfloat16)
        rows = per_group * (blocks - lag_block)
        source = x_ref[0, per_group * lag_block :, :]
        acc_ref[:rows, :] += jnp.dot(source, band, preferred_element_type=jnp.float32)
    for index in range(blocks):
        slab = acc_ref[per_group * index : per_group * (index + 1), :]
        o_ref[:, block * index : block * (index + 1)] = slab.astype(o_ref.dtype)


def correlate(grads, taps):
    tokens, channels = grads.shape
    groups = taps.shape[1]
    blocks = tokens // block
    shaped = grads.reshape(blocks, block, groups, per_group).transpose(2, 0, 3, 1)
    shaped = shaped.reshape(groups, blocks * per_group, block)
    reversed_taps = taps.astype(jnp.float32).T[:, ::-1]
    padded = jnp.concatenate([reversed_taps, jnp.zeros((groups, block), jnp.float32)], 1)
    padded = padded.reshape(groups, 1, tokens + block)
    flops = 2 * groups * per_group * block * block * blocks * (blocks + 1) // 2
    return pl.pallas_call(
        correlate_kernel,
        out_shape=jax.ShapeDtypeStruct((channels, tokens), jnp.bfloat16),
        grid=(groups,),
        in_specs=[
            pl.BlockSpec((1, blocks * per_group, block), lambda g: (g, 0, 0)),
            pl.BlockSpec((1, 1, tokens + block), lambda g: (g, 0, 0)),
        ],
        out_specs=pl.BlockSpec((per_group, tokens), lambda g: (g, 0)),
        scratch_shapes=[pltpu.VMEM((blocks * per_group, block), jnp.float32)],
        cost_estimate=pl.CostEstimate(
            flops=flops, bytes_accessed=grads.size * 4 + padded.size * 4, transcendentals=0
        ),
    )(shaped, padded)


def on_device(grad_out, qkv_saved, conv_saved, long_taps, short_taps):
    block_rows, channels = grad_out.shape
    out_wide = grad_out.astype(jnp.float32)
    query = qkv_saved[:, 0, :]
    key_part = qkv_saved[:, 1, :]
    value_part = qkv_saved[:, 2, :]
    grad_query = out_wide * conv_saved.astype(jnp.float32)
    grad_mixed = (out_wide * query.astype(jnp.float32)).astype(jnp.bfloat16)
    short_len = short_taps.shape[1]
    query_next = shifted(grad_query[: short_len - 1, None], "seq", -1)
    grad_mixed, query_next = lax.optimization_barrier((grad_mixed, query_next))
    mixed_cols = lax.all_to_all(grad_mixed, "seq", split_axis=1, concat_axis=0, tiled=True)
    taps_cols = lax.all_to_all(long_taps, "seq", split_axis=1, concat_axis=0, tiled=True)
    short_len = short_taps.shape[1]
    query_proj = short_filter(grad_query[:, None], short_taps[:1], block_rows, query_next)
    query_rows = spread_rows(query_proj, "chan")
    z_lanes = correlate(mixed_cols, taps_cols)
    z_lanes, query_rows = lax.optimization_barrier((z_lanes, query_rows))
    z_rows = lax.all_to_all(z_lanes, "seq", split_axis=1, concat_axis=0, tiled=True)
    z_wide = z_rows.astype(jnp.float32)
    grad_key = z_wide * value_part.T.astype(jnp.float32)
    grad_value = z_wide * key_part.T.astype(jnp.float32)
    count = lax.axis_size("chan")
    out = jnp.zeros((block_rows // count, 3, count * channels), jnp.bfloat16)
    for source, piece in query_rows:
        out = lax.dynamic_update_slice(out, piece, (0, 0, source * channels))
    for plane, lanes in ((1, grad_key), (2, grad_value)):
        filtered = lane_filter(lanes, short_taps[plane])
        for source, piece in spread_lanes(filtered, "chan"):
            out = lax.dynamic_update_slice(out, piece.T[:, None, :], (0, plane, source * channels))
    return out


def lane_filter(lanes, taps):
    block_rows = lanes.shape[1]
    short_len = taps.shape[0]
    borrowed = shifted(lanes[:, : short_len - 1], "seq", -1)
    extended = jnp.concatenate([lanes, borrowed], 1)
    result = jnp.zeros_like(lanes)
    for lag_index in range(short_len):
        result = result + taps[lag_index][:, None] * extended[:, lag_index : lag_index + block_rows]
    return result.astype(jnp.bfloat16)


def spread_lanes(value, axis):
    count = lax.axis_size(axis)
    me = lax.axis_index(axis)
    width = value.shape[1] // count

    def lanes_for(index):
        return lax.dynamic_slice_in_dim(value, pl.multiple_of(index * width, width), width, 1)

    pieces = [(me, lanes_for(me))]
    for step in range(1, count):
        pairs = [(source, (source + step) % count) for source in range(count)]
        outgoing = lanes_for((me + step) % count)
        pieces.append(((me + count - step) % count, lax.ppermute(outgoing, axis, pairs)))
    return pieces


def spread_rows(value, axis):
    count = lax.axis_size(axis)
    me = lax.axis_index(axis)
    rows, planes, channels = value.shape
    chunks = value.reshape(count, rows // count, planes, channels)
    pieces = [(me, lax.dynamic_index_in_dim(chunks, me, 0, keepdims=False))]
    for step in range(1, count):
        outgoing = lax.dynamic_index_in_dim(chunks, (me + step) % count, 0, keepdims=False)
        pairs = [(source, (source + step) % count) for source in range(count)]
        pieces.append(((me + count - step) % count, lax.ppermute(outgoing, axis, pairs)))
    return pieces


def place_rows(parts, count, rows, channels):
    planes = sum(pieces[0][1].shape[1] for pieces in parts)
    out = jnp.zeros((rows, planes, count * channels), parts[0][0][1].dtype)
    plane = 0
    for pieces in parts:
        for source, piece in pieces:
            out = lax.dynamic_update_slice(out, piece, (0, plane, source * channels))
        plane += pieces[0][1].shape[1]
    return out


def short_filter(stacked, taps, block_rows, borrowed):
    short_len = taps.shape[1]
    extended = jnp.concatenate([stacked, borrowed], 0)
    result = jnp.zeros_like(stacked)
    for lag_index in range(short_len):
        result = result + taps[:, lag_index, :][None] * extended[lag_index : lag_index + block_rows]
    return result.astype(jnp.bfloat16)


def solution(mesh):
    in_specs = (
        P("seq", "chan"),
        P("seq", None, "chan"),
        P("seq", "chan"),
        P("seq", "chan"),
        P(None, None, "chan"),
    )
    out_specs = P(("seq", "chan"), None, None)
    return jax.shard_map(
        on_device, mesh=mesh, in_specs=in_specs, out_specs=out_specs, check_vma=False
    )
```

```python
import functools

import jax
import jax.numpy as jnp
from jax import lax
from jax.experimental import pallas as pl
from jax.experimental.pallas import tpu as pltpu
from jax.sharding import PartitionSpec as P

block = 256
per_group = 16


def shifted(value, axis, steps):
    count = lax.axis_size(axis)
    leading, last = (max(0, -steps), min(count, count - steps))
    return lax.ppermute(value, axis, [(source, source + steps) for source in range(leading, last)])


def correlate_kernel(x_ref, h_ref, o_ref, acc_ref, rows_ref):
    tokens = x_ref.shape[1]
    blocks = tokens // block
    for index in range(blocks):
        rows_ref[per_group * index : per_group * (index + 1), :] = x_ref[:, block * index : block * (index + 1)]
    acc_ref[...] = jnp.zeros(acc_ref.shape, acc_ref.dtype)
    for lag_block in range(blocks):
        start = tokens - block * (lag_block + 1)
        window = h_ref[0, :, start : start + 2 * block]
        spread = jnp.broadcast_to(window, (block, 2 * block))
        rolled = pltpu.roll(spread, block + 1, 1, stride=1, stride_axis=0)
        band = rolled[:, :block].astype(jnp.bfloat16)
        rows = per_group * (blocks - lag_block)
        source = rows_ref[per_group * lag_block :, :]
        acc_ref[:rows, :] += jnp.dot(source, band, preferred_element_type=jnp.float32)
    for index in range(blocks):
        slab = acc_ref[per_group * index : per_group * (index + 1), :]
        o_ref[:, block * index : block * (index + 1)] = slab.astype(o_ref.dtype)


def correlate(grads, taps):
    channels, tokens = grads.shape
    groups = taps.shape[1]
    blocks = tokens // block
    reversed_taps = taps.astype(jnp.float32).T[:, ::-1]
    padded = jnp.concatenate([reversed_taps, jnp.zeros((groups, block), jnp.float32)], 1)
    padded = padded.reshape(groups, 1, tokens + block)
    flops = 2 * groups * per_group * block * block * blocks * (blocks + 1) // 2
    return pl.pallas_call(
        correlate_kernel,
        out_shape=jax.ShapeDtypeStruct((channels, tokens), jnp.bfloat16),
        grid=(groups,),
        in_specs=[
            pl.BlockSpec((per_group, tokens), lambda g: (g, 0)),
            pl.BlockSpec((1, 1, tokens + block), lambda g: (g, 0, 0)),
        ],
        out_specs=pl.BlockSpec((per_group, tokens), lambda g: (g, 0)),
        scratch_shapes=[
            pltpu.VMEM((blocks * per_group, block), jnp.float32),
            pltpu.VMEM((blocks * per_group, block), jnp.bfloat16),
        ],
        cost_estimate=pl.CostEstimate(
            flops=flops, bytes_accessed=grads.size * 4 + padded.size * 4, transcendentals=0
        ),
    )(grads, padded)


def on_device(grad_out, qkv_saved, conv_saved, long_taps, short_taps):
    block_rows, channels = grad_out.shape
    out_wide = grad_out.astype(jnp.float32)
    query = qkv_saved[:, 0, :]
    key_part = qkv_saved[:, 1, :]
    value_part = qkv_saved[:, 2, :]
    grad_query = out_wide * conv_saved.astype(jnp.float32)
    grad_mixed = (out_wide * query.astype(jnp.float32)).astype(jnp.bfloat16)
    short_len = short_taps.shape[1]
    query_next = shifted(grad_query[: short_len - 1, None], "seq", -1)
    grad_mixed, query_next = lax.optimization_barrier((grad_mixed, query_next))
    mixed_cols = lax.all_to_all(grad_mixed.T, "seq", split_axis=0, concat_axis=1, tiled=True)
    taps_cols = lax.all_to_all(long_taps, "seq", split_axis=1, concat_axis=0, tiled=True)
    short_len = short_taps.shape[1]
    query_proj = short_filter(grad_query[:, None], short_taps[:1], block_rows, query_next)
    query_rows = spread_rows(query_proj, "chan")
    z_lanes = correlate(mixed_cols, taps_cols)
    z_lanes, query_rows = lax.optimization_barrier((z_lanes, query_rows))
    z_rows = lax.all_to_all(z_lanes, "seq", split_axis=1, concat_axis=0, tiled=True)
    z_wide = z_rows.astype(jnp.float32)
    grad_key = z_wide * value_part.T.astype(jnp.float32)
    grad_value = z_wide * key_part.T.astype(jnp.float32)
    count = lax.axis_size("chan")
    out = jnp.zeros((block_rows // count, 3, count * channels), jnp.bfloat16)
    for source, piece in query_rows:
        out = lax.dynamic_update_slice(out, piece, (0, 0, source * channels))
    for plane, lanes in ((1, grad_key), (2, grad_value)):
        filtered = lane_filter(lanes, short_taps[plane])
        for source, piece in spread_lanes(filtered, "chan"):
            out = lax.dynamic_update_slice(out, piece.T[:, None, :], (0, plane, source * channels))
    return out


def lane_filter(lanes, taps):
    block_rows = lanes.shape[1]
    short_len = taps.shape[0]
    borrowed = shifted(lanes[:, : short_len - 1], "seq", -1)
    extended = jnp.concatenate([lanes, borrowed], 1)
    result = jnp.zeros_like(lanes)
    for lag_index in range(short_len):
        result = result + taps[lag_index][:, None] * extended[:, lag_index : lag_index + block_rows]
    return result.astype(jnp.bfloat16)


def spread_lanes(value, axis):
    count = lax.axis_size(axis)
    me = lax.axis_index(axis)
    width = value.shape[1] // count

    def lanes_for(index):
        return lax.dynamic_slice_in_dim(value, pl.multiple_of(index * width, width), width, 1)

    pieces = [(me, lanes_for(me))]
    for step in range(1, count):
        pairs = [(source, (source + step) % count) for source in range(count)]
        outgoing = lanes_for((me + step) % count)
        pieces.append(((me + count - step) % count, lax.ppermute(outgoing, axis, pairs)))
    return pieces


def spread_rows(value, axis):
    count = lax.axis_size(axis)
    me = lax.axis_index(axis)
    rows, planes, channels = value.shape
    chunks = value.reshape(count, rows // count, planes, channels)
    pieces = [(me, lax.dynamic_index_in_dim(chunks, me, 0, keepdims=False))]
    for step in range(1, count):
        outgoing = lax.dynamic_index_in_dim(chunks, (me + step) % count, 0, keepdims=False)
        pairs = [(source, (source + step) % count) for source in range(count)]
        pieces.append(((me + count - step) % count, lax.ppermute(outgoing, axis, pairs)))
    return pieces


def place_rows(parts, count, rows, channels):
    planes = sum(pieces[0][1].shape[1] for pieces in parts)
    out = jnp.zeros((rows, planes, count * channels), parts[0][0][1].dtype)
    plane = 0
    for pieces in parts:
        for source, piece in pieces:
            out = lax.dynamic_update_slice(out, piece, (0, plane, source * channels))
        plane += pieces[0][1].shape[1]
    return out


def short_filter(stacked, taps, block_rows, borrowed):
    short_len = taps.shape[1]
    extended = jnp.concatenate([stacked, borrowed], 0)
    result = jnp.zeros_like(stacked)
    for lag_index in range(short_len):
        result = result + taps[:, lag_index, :][None] * extended[lag_index : lag_index + block_rows]
    return result.astype(jnp.bfloat16)


def solution(mesh):
    in_specs = (
        P("seq", "chan"),
        P("seq", None, "chan"),
        P("seq", "chan"),
        P("seq", "chan"),
        P(None, None, "chan"),
    )
    out_specs = P(("seq", "chan"), None, None)
    return jax.shard_map(
        on_device, mesh=mesh, in_specs=in_specs, out_specs=out_specs, check_vma=False
    )
```

```python
import functools

import jax
import jax.numpy as jnp
from jax import lax
from jax.experimental import pallas as pl
from jax.experimental.pallas import tpu as pltpu
from jax.sharding import PartitionSpec as P

block = 256
per_group = 16


def shifted(value, axis, steps):
    count = lax.axis_size(axis)
    leading, last = (max(0, -steps), min(count, count - steps))
    return lax.ppermute(value, axis, [(source, source + steps) for source in range(leading, last)])


def correlate_kernel(x_ref, h_ref, o_ref, acc_ref, rows_ref):
    tokens = x_ref.shape[1]
    blocks = tokens // block
    for index in range(blocks):
        rows_ref[per_group * index : per_group * (index + 1), :] = x_ref[:, block * index : block * (index + 1)]
    acc_ref[...] = jnp.zeros(acc_ref.shape, acc_ref.dtype)
    for lag_block in range(blocks):
        start = tokens - block * (lag_block + 1)
        window = h_ref[0, :, start : start + 2 * block]
        spread = jnp.broadcast_to(window, (block, 2 * block))
        rolled = pltpu.roll(spread, block + 1, 1, stride=1, stride_axis=0)
        band = rolled[:, :block].astype(jnp.bfloat16)
        rows = per_group * (blocks - lag_block)
        source = rows_ref[per_group * lag_block :, :]
        acc_ref[:rows, :] += jnp.dot(source, band, preferred_element_type=jnp.float32)
    for index in range(blocks):
        slab = acc_ref[per_group * index : per_group * (index + 1), :]
        o_ref[:, block * index : block * (index + 1)] = slab.astype(o_ref.dtype)


def correlate(grads, taps):
    channels, tokens = grads.shape
    groups = taps.shape[1]
    blocks = tokens // block
    reversed_taps = taps.astype(jnp.float32).T[:, ::-1]
    padded = jnp.concatenate([reversed_taps, jnp.zeros((groups, block), jnp.float32)], 1)
    padded = padded.reshape(groups, 1, tokens + block)
    flops = 2 * groups * per_group * block * block * blocks * (blocks + 1) // 2
    return pl.pallas_call(
        correlate_kernel,
        out_shape=jax.ShapeDtypeStruct((channels, tokens), jnp.bfloat16),
        grid=(groups,),
        in_specs=[
            pl.BlockSpec((per_group, tokens), lambda g: (g, 0)),
            pl.BlockSpec((1, 1, tokens + block), lambda g: (g, 0, 0)),
        ],
        out_specs=pl.BlockSpec((per_group, tokens), lambda g: (g, 0)),
        scratch_shapes=[
            pltpu.VMEM((blocks * per_group, block), jnp.float32),
            pltpu.VMEM((blocks * per_group, block), jnp.bfloat16),
        ],
        cost_estimate=pl.CostEstimate(
            flops=flops, bytes_accessed=grads.size * 4 + padded.size * 4, transcendentals=0
        ),
    )(grads, padded)


def on_device(grad_out, qkv_saved, conv_saved, long_taps, short_taps):
    block_rows, channels = grad_out.shape
    out_wide = grad_out.astype(jnp.float32)
    query = qkv_saved[:, 0, :]
    key_part = qkv_saved[:, 1, :]
    value_part = qkv_saved[:, 2, :]
    grad_query = out_wide * conv_saved.astype(jnp.float32)
    grad_mixed = (out_wide * query.astype(jnp.float32)).astype(jnp.bfloat16)
    short_len = short_taps.shape[1]
    query_next = shifted(grad_query[: short_len - 1, None], "seq", -1)
    grad_mixed, query_next = lax.optimization_barrier((grad_mixed, query_next))
    mixed_cols = lax.all_to_all(grad_mixed.T, "seq", split_axis=0, concat_axis=1, tiled=True)
    taps_cols = lax.all_to_all(long_taps, "seq", split_axis=1, concat_axis=0, tiled=True)
    short_len = short_taps.shape[1]
    query_proj = short_filter(grad_query[:, None], short_taps[:1], block_rows, query_next)
    query_rows = spread_rows(query_proj, "chan")
    halves = 2
    part = mixed_cols.shape[0] // halves
    group_part = taps_cols.shape[1] // halves
    returned = []
    for half in range(halves):
        z_lanes = correlate(
            mixed_cols[half * part : (half + 1) * part],
            taps_cols[:, half * group_part : (half + 1) * group_part],
        )
        if half == 0:
            z_lanes, query_rows = lax.optimization_barrier((z_lanes, query_rows))
        returned.append(lax.all_to_all(z_lanes, "seq", split_axis=1, concat_axis=0, tiled=True))
    shards = lax.axis_size("seq")
    z_rows = jnp.stack([piece.reshape(shards, part, -1) for piece in returned], 1)
    z_rows = z_rows.reshape(shards * halves * part, -1)
    z_wide = z_rows.astype(jnp.float32)
    grad_key = z_wide * value_part.T.astype(jnp.float32)
    grad_value = z_wide * key_part.T.astype(jnp.float32)
    count = lax.axis_size("chan")
    out = jnp.zeros((block_rows // count, 3, count * channels), jnp.bfloat16)
    for source, piece in query_rows:
        out = lax.dynamic_update_slice(out, piece, (0, 0, source * channels))
    for plane, lanes in ((1, grad_key), (2, grad_value)):
        filtered = lane_filter(lanes, short_taps[plane])
        for source, piece in spread_lanes(filtered, "chan"):
            out = lax.dynamic_update_slice(out, piece.T[:, None, :], (0, plane, source * channels))
    return out


def lane_filter(lanes, taps):
    block_rows = lanes.shape[1]
    short_len = taps.shape[0]
    borrowed = shifted(lanes[:, : short_len - 1], "seq", -1)
    extended = jnp.concatenate([lanes, borrowed], 1)
    result = jnp.zeros_like(lanes)
    for lag_index in range(short_len):
        result = result + taps[lag_index][:, None] * extended[:, lag_index : lag_index + block_rows]
    return result.astype(jnp.bfloat16)


def spread_lanes(value, axis):
    count = lax.axis_size(axis)
    me = lax.axis_index(axis)
    width = value.shape[1] // count

    def lanes_for(index):
        return lax.dynamic_slice_in_dim(value, pl.multiple_of(index * width, width), width, 1)

    pieces = [(me, lanes_for(me))]
    for step in range(1, count):
        pairs = [(source, (source + step) % count) for source in range(count)]
        outgoing = lanes_for((me + step) % count)
        pieces.append(((me + count - step) % count, lax.ppermute(outgoing, axis, pairs)))
    return pieces


def spread_rows(value, axis):
    count = lax.axis_size(axis)
    me = lax.axis_index(axis)
    rows, planes, channels = value.shape
    chunks = value.reshape(count, rows // count, planes, channels)
    pieces = [(me, lax.dynamic_index_in_dim(chunks, me, 0, keepdims=False))]
    for step in range(1, count):
        outgoing = lax.dynamic_index_in_dim(chunks, (me + step) % count, 0, keepdims=False)
        pairs = [(source, (source + step) % count) for source in range(count)]
        pieces.append(((me + count - step) % count, lax.ppermute(outgoing, axis, pairs)))
    return pieces


def place_rows(parts, count, rows, channels):
    planes = sum(pieces[0][1].shape[1] for pieces in parts)
    out = jnp.zeros((rows, planes, count * channels), parts[0][0][1].dtype)
    plane = 0
    for pieces in parts:
        for source, piece in pieces:
            out = lax.dynamic_update_slice(out, piece, (0, plane, source * channels))
        plane += pieces[0][1].shape[1]
    return out


def short_filter(stacked, taps, block_rows, borrowed):
    short_len = taps.shape[1]
    extended = jnp.concatenate([stacked, borrowed], 0)
    result = jnp.zeros_like(stacked)
    for lag_index in range(short_len):
        result = result + taps[:, lag_index, :][None] * extended[lag_index : lag_index + block_rows]
    return result.astype(jnp.bfloat16)


def solution(mesh):
    in_specs = (
        P("seq", "chan"),
        P("seq", None, "chan"),
        P("seq", "chan"),
        P("seq", "chan"),
        P(None, None, "chan"),
    )
    out_specs = P(("seq", "chan"), None, None)
    return jax.shard_map(
        on_device, mesh=mesh, in_specs=in_specs, out_specs=out_specs, check_vma=False
    )
```

```python
import functools

import jax
import jax.numpy as jnp
from jax import lax
from jax.experimental import pallas as pl
from jax.experimental.pallas import tpu as pltpu
from jax.sharding import PartitionSpec as P

block = 256
per_group = 16


def shifted(value, axis, steps):
    count = lax.axis_size(axis)
    leading, last = (max(0, -steps), min(count, count - steps))
    return lax.ppermute(value, axis, [(source, source + steps) for source in range(leading, last)])


def correlate_kernel(x_ref, h_ref, o_ref, acc_ref, rows_ref):
    tokens = x_ref.shape[1]
    blocks = tokens // block
    for index in range(blocks):
        rows_ref[per_group * index : per_group * (index + 1), :] = x_ref[:, block * index : block * (index + 1)]
    acc_ref[...] = jnp.zeros(acc_ref.shape, acc_ref.dtype)
    for lag_block in range(blocks):
        start = tokens - block * (lag_block + 1)
        window = h_ref[0, :, start : start + 2 * block]
        spread = jnp.broadcast_to(window, (block, 2 * block))
        rolled = pltpu.roll(spread, block + 1, 1, stride=1, stride_axis=0)
        band = rolled[:, :block].astype(jnp.bfloat16)
        rows = per_group * (blocks - lag_block)
        source = rows_ref[per_group * lag_block :, :]
        acc_ref[:rows, :] += jnp.dot(source, band, preferred_element_type=jnp.float32)
    for index in range(blocks):
        slab = acc_ref[per_group * index : per_group * (index + 1), :]
        o_ref[:, block * index : block * (index + 1)] = slab.astype(o_ref.dtype)


def correlate(grads, taps):
    channels, tokens = grads.shape
    groups = taps.shape[0]
    blocks = tokens // block
    reversed_taps = taps.astype(jnp.float32)[:, ::-1]
    padded = jnp.concatenate([reversed_taps, jnp.zeros((groups, block), jnp.float32)], 1)
    padded = padded.reshape(groups, 1, tokens + block)
    flops = 2 * groups * per_group * block * block * blocks * (blocks + 1) // 2
    return pl.pallas_call(
        correlate_kernel,
        out_shape=jax.ShapeDtypeStruct((channels, tokens), jnp.bfloat16),
        grid=(groups,),
        in_specs=[
            pl.BlockSpec((per_group, tokens), lambda g: (g, 0)),
            pl.BlockSpec((1, 1, tokens + block), lambda g: (g, 0, 0)),
        ],
        out_specs=pl.BlockSpec((per_group, tokens), lambda g: (g, 0)),
        scratch_shapes=[
            pltpu.VMEM((blocks * per_group, block), jnp.float32),
            pltpu.VMEM((blocks * per_group, block), jnp.bfloat16),
        ],
        cost_estimate=pl.CostEstimate(
            flops=flops, bytes_accessed=grads.size * 4 + padded.size * 4, transcendentals=0
        ),
    )(grads, padded)


def on_device(grad_out, qkv_saved, conv_saved, long_taps, short_taps):
    block_rows, channels = grad_out.shape
    out_wide = grad_out.astype(jnp.float32)
    query = qkv_saved[:, 0, :]
    key_part = qkv_saved[:, 1, :]
    value_part = qkv_saved[:, 2, :]
    grad_query = out_wide * conv_saved.astype(jnp.float32)
    grad_mixed = (out_wide * query.astype(jnp.float32)).astype(jnp.bfloat16)
    short_len = short_taps.shape[1]
    query_next = shifted(grad_query[: short_len - 1, None], "seq", -1)
    grad_mixed, query_next = lax.optimization_barrier((grad_mixed, query_next))
    shards = lax.axis_size("seq")
    mixed_parts = grad_mixed.T.reshape(shards, -1, block_rows)
    taps_parts = long_taps.T.reshape(shards, -1, block_rows)
    width = mixed_parts.shape[1]
    joined = jnp.concatenate([mixed_parts, taps_parts], 1)
    joined = lax.all_to_all(joined, "seq", split_axis=0, concat_axis=0, tiled=True)
    mixed_cols = joined[:, :width].transpose(1, 0, 2).reshape(width, shards * block_rows)
    taps_cols = joined[:, width:].transpose(1, 0, 2).reshape(-1, shards * block_rows)
    short_len = short_taps.shape[1]
    query_proj = short_filter(grad_query[:, None], short_taps[:1], block_rows, query_next)
    query_rows = spread_rows(query_proj, "chan")
    z_lanes = correlate(mixed_cols, taps_cols)
    z_lanes, query_rows = lax.optimization_barrier((z_lanes, query_rows))
    z_rows = lax.all_to_all(z_lanes, "seq", split_axis=1, concat_axis=0, tiled=True)
    z_wide = z_rows.astype(jnp.float32)
    grad_key = z_wide * value_part.T.astype(jnp.float32)
    grad_value = z_wide * key_part.T.astype(jnp.float32)
    count = lax.axis_size("chan")
    out = jnp.zeros((block_rows // count, 3, count * channels), jnp.bfloat16)
    for source, piece in query_rows:
        out = lax.dynamic_update_slice(out, piece, (0, 0, source * channels))
    for plane, lanes in ((1, grad_key), (2, grad_value)):
        filtered = lane_filter(lanes, short_taps[plane])
        for source, piece in spread_lanes(filtered, "chan"):
            out = lax.dynamic_update_slice(out, piece.T[:, None, :], (0, plane, source * channels))
    return out


def lane_filter(lanes, taps):
    block_rows = lanes.shape[1]
    short_len = taps.shape[0]
    borrowed = shifted(lanes[:, : short_len - 1], "seq", -1)
    extended = jnp.concatenate([lanes, borrowed], 1)
    result = jnp.zeros_like(lanes)
    for lag_index in range(short_len):
        result = result + taps[lag_index][:, None] * extended[:, lag_index : lag_index + block_rows]
    return result.astype(jnp.bfloat16)


def spread_lanes(value, axis):
    count = lax.axis_size(axis)
    me = lax.axis_index(axis)
    width = value.shape[1] // count

    def lanes_for(index):
        return lax.dynamic_slice_in_dim(value, pl.multiple_of(index * width, width), width, 1)

    pieces = [(me, lanes_for(me))]
    for step in range(1, count):
        pairs = [(source, (source + step) % count) for source in range(count)]
        outgoing = lanes_for((me + step) % count)
        pieces.append(((me + count - step) % count, lax.ppermute(outgoing, axis, pairs)))
    return pieces


def spread_rows(value, axis):
    count = lax.axis_size(axis)
    me = lax.axis_index(axis)
    rows, planes, channels = value.shape
    chunks = value.reshape(count, rows // count, planes, channels)
    pieces = [(me, lax.dynamic_index_in_dim(chunks, me, 0, keepdims=False))]
    for step in range(1, count):
        outgoing = lax.dynamic_index_in_dim(chunks, (me + step) % count, 0, keepdims=False)
        pairs = [(source, (source + step) % count) for source in range(count)]
        pieces.append(((me + count - step) % count, lax.ppermute(outgoing, axis, pairs)))
    return pieces


def place_rows(parts, count, rows, channels):
    planes = sum(pieces[0][1].shape[1] for pieces in parts)
    out = jnp.zeros((rows, planes, count * channels), parts[0][0][1].dtype)
    plane = 0
    for pieces in parts:
        for source, piece in pieces:
            out = lax.dynamic_update_slice(out, piece, (0, plane, source * channels))
        plane += pieces[0][1].shape[1]
    return out


def short_filter(stacked, taps, block_rows, borrowed):
    short_len = taps.shape[1]
    extended = jnp.concatenate([stacked, borrowed], 0)
    result = jnp.zeros_like(stacked)
    for lag_index in range(short_len):
        result = result + taps[:, lag_index, :][None] * extended[lag_index : lag_index + block_rows]
    return result.astype(jnp.bfloat16)


def solution(mesh):
    in_specs = (
        P("seq", "chan"),
        P("seq", None, "chan"),
        P("seq", "chan"),
        P("seq", "chan"),
        P(None, None, "chan"),
    )
    out_specs = P(("seq", "chan"), None, None)
    return jax.shard_map(
        on_device, mesh=mesh, in_specs=in_specs, out_specs=out_specs, check_vma=False
    )
```

```python
import functools

import jax
import jax.numpy as jnp
from jax import lax
from jax.experimental import pallas as pl
from jax.experimental.pallas import tpu as pltpu
from jax.sharding import PartitionSpec as P

block = 256
per_group = 16


def shifted(value, axis, steps):
    count = lax.axis_size(axis)
    leading, last = (max(0, -steps), min(count, count - steps))
    return lax.ppermute(value, axis, [(source, source + steps) for source in range(leading, last)])


def correlate_kernel(x_ref, h_ref, o_ref, acc_ref, rows_ref):
    tokens = x_ref.shape[1]
    blocks = tokens // block
    for index in range(blocks):
        rows_ref[per_group * index : per_group * (index + 1), :] = x_ref[:, block * index : block * (index + 1)]
    acc_ref[...] = jnp.zeros(acc_ref.shape, acc_ref.dtype)
    lag_block = 0
    while lag_block < blocks:
        paired = 2 if lag_block + 1 < blocks else 1
        start = tokens - block * (lag_block + paired)
        window = h_ref[0, :, start : start + (paired + 1) * block]
        spread = jnp.broadcast_to(window, (block, (paired + 1) * block))
        rolled = pltpu.roll(spread, paired * block + 1, 1, stride=1, stride_axis=0)
        for offset in range(paired):
            band = rolled[:, (paired - 1 - offset) * block : (paired - offset) * block]
            band = band.astype(jnp.bfloat16)
            rows = per_group * (blocks - lag_block - offset)
            source = rows_ref[per_group * (lag_block + offset) :, :]
            acc_ref[:rows, :] += jnp.dot(source, band, preferred_element_type=jnp.float32)
        lag_block += paired
    for index in range(blocks):
        slab = acc_ref[per_group * index : per_group * (index + 1), :]
        o_ref[:, block * index : block * (index + 1)] = slab.astype(o_ref.dtype)


def correlate(grads, taps):
    channels, tokens = grads.shape
    groups = taps.shape[1]
    blocks = tokens // block
    reversed_taps = taps.astype(jnp.float32).T[:, ::-1]
    padded = jnp.concatenate([reversed_taps, jnp.zeros((groups, block), jnp.float32)], 1)
    padded = padded.reshape(groups, 1, tokens + block)
    flops = 2 * groups * per_group * block * block * blocks * (blocks + 1) // 2
    return pl.pallas_call(
        correlate_kernel,
        out_shape=jax.ShapeDtypeStruct((channels, tokens), jnp.bfloat16),
        grid=(groups,),
        in_specs=[
            pl.BlockSpec((per_group, tokens), lambda g: (g, 0)),
            pl.BlockSpec((1, 1, tokens + block), lambda g: (g, 0, 0)),
        ],
        out_specs=pl.BlockSpec((per_group, tokens), lambda g: (g, 0)),
        scratch_shapes=[
            pltpu.VMEM((blocks * per_group, block), jnp.float32),
            pltpu.VMEM((blocks * per_group, block), jnp.bfloat16),
        ],
        cost_estimate=pl.CostEstimate(
            flops=flops, bytes_accessed=grads.size * 4 + padded.size * 4, transcendentals=0
        ),
    )(grads, padded)


def on_device(grad_out, qkv_saved, conv_saved, long_taps, short_taps):
    block_rows, channels = grad_out.shape
    out_wide = grad_out.astype(jnp.float32)
    query = qkv_saved[:, 0, :]
    key_part = qkv_saved[:, 1, :]
    value_part = qkv_saved[:, 2, :]
    grad_query = out_wide * conv_saved.astype(jnp.float32)
    grad_mixed = (out_wide * query.astype(jnp.float32)).astype(jnp.bfloat16)
    short_len = short_taps.shape[1]
    query_next = shifted(grad_query[: short_len - 1, None], "seq", -1)
    grad_mixed, query_next = lax.optimization_barrier((grad_mixed, query_next))
    mixed_cols = lax.all_to_all(grad_mixed.T, "seq", split_axis=0, concat_axis=1, tiled=True)
    taps_cols = lax.all_to_all(long_taps, "seq", split_axis=1, concat_axis=0, tiled=True)
    short_len = short_taps.shape[1]
    query_proj = short_filter(grad_query[:, None], short_taps[:1], block_rows, query_next)
    query_rows = spread_rows(query_proj, "chan")
    z_lanes = correlate(mixed_cols, taps_cols)
    z_lanes, query_rows = lax.optimization_barrier((z_lanes, query_rows))
    z_rows = lax.all_to_all(z_lanes, "seq", split_axis=1, concat_axis=0, tiled=True)
    z_wide = z_rows.astype(jnp.float32)
    grad_key = z_wide * value_part.T.astype(jnp.float32)
    grad_value = z_wide * key_part.T.astype(jnp.float32)
    count = lax.axis_size("chan")
    out = jnp.zeros((block_rows // count, 3, count * channels), jnp.bfloat16)
    for source, piece in query_rows:
        out = lax.dynamic_update_slice(out, piece, (0, 0, source * channels))
    for plane, lanes in ((1, grad_key), (2, grad_value)):
        filtered = lane_filter(lanes, short_taps[plane])
        for source, piece in spread_lanes(filtered, "chan"):
            out = lax.dynamic_update_slice(out, piece.T[:, None, :], (0, plane, source * channels))
    return out


def lane_filter(lanes, taps):
    block_rows = lanes.shape[1]
    short_len = taps.shape[0]
    borrowed = shifted(lanes[:, : short_len - 1], "seq", -1)
    extended = jnp.concatenate([lanes, borrowed], 1)
    result = jnp.zeros_like(lanes)
    for lag_index in range(short_len):
        result = result + taps[lag_index][:, None] * extended[:, lag_index : lag_index + block_rows]
    return result.astype(jnp.bfloat16)


def spread_lanes(value, axis):
    count = lax.axis_size(axis)
    me = lax.axis_index(axis)
    width = value.shape[1] // count

    def lanes_for(index):
        return lax.dynamic_slice_in_dim(value, pl.multiple_of(index * width, width), width, 1)

    pieces = [(me, lanes_for(me))]
    for step in range(1, count):
        pairs = [(source, (source + step) % count) for source in range(count)]
        outgoing = lanes_for((me + step) % count)
        pieces.append(((me + count - step) % count, lax.ppermute(outgoing, axis, pairs)))
    return pieces


def spread_rows(value, axis):
    count = lax.axis_size(axis)
    me = lax.axis_index(axis)
    rows, planes, channels = value.shape
    chunks = value.reshape(count, rows // count, planes, channels)
    pieces = [(me, lax.dynamic_index_in_dim(chunks, me, 0, keepdims=False))]
    for step in range(1, count):
        outgoing = lax.dynamic_index_in_dim(chunks, (me + step) % count, 0, keepdims=False)
        pairs = [(source, (source + step) % count) for source in range(count)]
        pieces.append(((me + count - step) % count, lax.ppermute(outgoing, axis, pairs)))
    return pieces


def place_rows(parts, count, rows, channels):
    planes = sum(pieces[0][1].shape[1] for pieces in parts)
    out = jnp.zeros((rows, planes, count * channels), parts[0][0][1].dtype)
    plane = 0
    for pieces in parts:
        for source, piece in pieces:
            out = lax.dynamic_update_slice(out, piece, (0, plane, source * channels))
        plane += pieces[0][1].shape[1]
    return out


def short_filter(stacked, taps, block_rows, borrowed):
    short_len = taps.shape[1]
    extended = jnp.concatenate([stacked, borrowed], 0)
    result = jnp.zeros_like(stacked)
    for lag_index in range(short_len):
        result = result + taps[:, lag_index, :][None] * extended[lag_index : lag_index + block_rows]
    return result.astype(jnp.bfloat16)


def solution(mesh):
    in_specs = (
        P("seq", "chan"),
        P("seq", None, "chan"),
        P("seq", "chan"),
        P("seq", "chan"),
        P(None, None, "chan"),
    )
    out_specs = P(("seq", "chan"), None, None)
    return jax.shard_map(
        on_device, mesh=mesh, in_specs=in_specs, out_specs=out_specs, check_vma=False
    )
```

```python
import functools

import jax
import jax.numpy as jnp
from jax import lax
from jax.experimental import pallas as pl
from jax.experimental.pallas import tpu as pltpu
from jax.sharding import PartitionSpec as P

block = 256
per_group = 16


def shifted(value, axis, steps):
    count = lax.axis_size(axis)
    leading, last = (max(0, -steps), min(count, count - steps))
    return lax.ppermute(value, axis, [(source, source + steps) for source in range(leading, last)])


def correlate_kernel(x_ref, h_ref, o_ref, acc_ref, rows_ref):
    tokens = x_ref.shape[1]
    blocks = tokens // block
    for index in range(blocks):
        rows_ref[per_group * index : per_group * (index + 1), :] = x_ref[:, block * index : block * (index + 1)]
    acc_ref[...] = jnp.zeros(acc_ref.shape, acc_ref.dtype)
    for lag_block in range(blocks):
        start = tokens - block * (lag_block + 1)
        window = h_ref[0, :, start : start + 2 * block]
        spread = jnp.broadcast_to(window, (block, 2 * block))
        rolled = pltpu.roll(spread, block + 1, 1, stride=1, stride_axis=0)
        band = rolled[:, :block].astype(jnp.bfloat16)
        rows = per_group * (blocks - lag_block)
        source = rows_ref[per_group * lag_block :, :]
        acc_ref[:rows, :] += jnp.dot(source, band, preferred_element_type=jnp.float32)
    for index in range(blocks):
        slab = acc_ref[per_group * index : per_group * (index + 1), :]
        o_ref[:, block * index : block * (index + 1)] = slab.astype(o_ref.dtype)


def correlate(grads, taps):
    channels, tokens = grads.shape
    groups = taps.shape[1]
    blocks = tokens // block
    reversed_taps = taps.astype(jnp.float32).T[:, ::-1]
    padded = jnp.concatenate([reversed_taps, jnp.zeros((groups, block), jnp.float32)], 1)
    padded = padded.reshape(groups, 1, tokens + block)
    flops = 2 * groups * per_group * block * block * blocks * (blocks + 1) // 2
    return pl.pallas_call(
        correlate_kernel,
        out_shape=jax.ShapeDtypeStruct((channels, tokens), jnp.bfloat16),
        grid=(groups,),
        in_specs=[
            pl.BlockSpec((per_group, tokens), lambda g: (g, 0)),
            pl.BlockSpec((1, 1, tokens + block), lambda g: (g, 0, 0)),
        ],
        out_specs=pl.BlockSpec((per_group, tokens), lambda g: (g, 0)),
        scratch_shapes=[
            pltpu.VMEM((blocks * per_group, block), jnp.float32),
            pltpu.VMEM((blocks * per_group, block), jnp.bfloat16),
        ],
        cost_estimate=pl.CostEstimate(
            flops=flops, bytes_accessed=grads.size * 4 + padded.size * 4, transcendentals=0
        ),
    )(grads, padded)


def on_device(grad_out, qkv_saved, conv_saved, long_taps, short_taps):
    block_rows, channels = grad_out.shape
    out_wide = grad_out.astype(jnp.float32)
    query = qkv_saved[:, 0, :]
    key_part = qkv_saved[:, 1, :]
    value_part = qkv_saved[:, 2, :]
    grad_query = out_wide * conv_saved.astype(jnp.float32)
    grad_mixed = (out_wide * query.astype(jnp.float32)).astype(jnp.bfloat16)
    short_len = short_taps.shape[1]
    query_next = shifted(grad_query[: short_len - 1, None], "seq", -1)
    grad_mixed, query_next = lax.optimization_barrier((grad_mixed, query_next))
    mixed_cols = lax.all_to_all(grad_mixed.T, "seq", split_axis=0, concat_axis=1, tiled=True)
    taps_cols = lax.all_to_all(long_taps, "seq", split_axis=1, concat_axis=0, tiled=True)
    short_len = short_taps.shape[1]
    query_proj = short_filter(grad_query[:, None], short_taps[:1], block_rows, query_next)
    query_rows = spread_rows(query_proj, "chan")
    z_lanes = correlate(mixed_cols, taps_cols)
    z_lanes, query_rows = lax.optimization_barrier((z_lanes, query_rows))
    z_rows = lax.all_to_all(z_lanes, "seq", split_axis=1, concat_axis=0, tiled=True)
    z_wide = z_rows.astype(jnp.float32)
    grad_key = z_wide * lanes_first(value_part)
    grad_value = z_wide * lanes_first(key_part)
    count = lax.axis_size("chan")
    out = jnp.zeros((block_rows // count, 3, count * channels), jnp.bfloat16)
    for source, piece in query_rows:
        out = lax.dynamic_update_slice(out, piece, (0, 0, source * channels))
    for plane, lanes in ((1, grad_key), (2, grad_value)):
        filtered = lane_filter(lanes, short_taps[plane])
        for source, piece in spread_lanes(filtered, "chan"):
            out = lax.dynamic_update_slice(out, piece.T[:, None, :], (0, plane, source * channels))
    return out


def transpose_kernel(x_ref, o_ref):
    o_ref[...] = x_ref[...].astype(jnp.float32).T


def lanes_first(rows):
    count, width = rows.shape
    return pl.pallas_call(
        transpose_kernel,
        out_shape=jax.ShapeDtypeStruct((width, count), jnp.float32),
        grid=(width // block,),
        in_specs=[pl.BlockSpec((count, block), lambda j: (0, j))],
        out_specs=pl.BlockSpec((block, count), lambda j: (j, 0)),
    )(rows)


def lane_filter(lanes, taps):
    block_rows = lanes.shape[1]
    short_len = taps.shape[0]
    borrowed = shifted(lanes[:, : short_len - 1], "seq", -1)
    extended = jnp.concatenate([lanes, borrowed], 1)
    result = jnp.zeros_like(lanes)
    for lag_index in range(short_len):
        result = result + taps[lag_index][:, None] * extended[:, lag_index : lag_index + block_rows]
    return result.astype(jnp.bfloat16)


def spread_lanes(value, axis):
    count = lax.axis_size(axis)
    me = lax.axis_index(axis)
    width = value.shape[1] // count

    def lanes_for(index):
        return lax.dynamic_slice_in_dim(value, pl.multiple_of(index * width, width), width, 1)

    pieces = [(me, lanes_for(me))]
    for step in range(1, count):
        pairs = [(source, (source + step) % count) for source in range(count)]
        outgoing = lanes_for((me + step) % count)
        pieces.append(((me + count - step) % count, lax.ppermute(outgoing, axis, pairs)))
    return pieces


def spread_rows(value, axis):
    count = lax.axis_size(axis)
    me = lax.axis_index(axis)
    rows, planes, channels = value.shape
    chunks = value.reshape(count, rows // count, planes, channels)
    pieces = [(me, lax.dynamic_index_in_dim(chunks, me, 0, keepdims=False))]
    for step in range(1, count):
        outgoing = lax.dynamic_index_in_dim(chunks, (me + step) % count, 0, keepdims=False)
        pairs = [(source, (source + step) % count) for source in range(count)]
        pieces.append(((me + count - step) % count, lax.ppermute(outgoing, axis, pairs)))
    return pieces


def place_rows(parts, count, rows, channels):
    planes = sum(pieces[0][1].shape[1] for pieces in parts)
    out = jnp.zeros((rows, planes, count * channels), parts[0][0][1].dtype)
    plane = 0
    for pieces in parts:
        for source, piece in pieces:
            out = lax.dynamic_update_slice(out, piece, (0, plane, source * channels))
        plane += pieces[0][1].shape[1]
    return out


def short_filter(stacked, taps, block_rows, borrowed):
    short_len = taps.shape[1]
    extended = jnp.concatenate([stacked, borrowed], 0)
    result = jnp.zeros_like(stacked)
    for lag_index in range(short_len):
        result = result + taps[:, lag_index, :][None] * extended[lag_index : lag_index + block_rows]
    return result.astype(jnp.bfloat16)


def solution(mesh):
    in_specs = (
        P("seq", "chan"),
        P("seq", None, "chan"),
        P("seq", "chan"),
        P("seq", "chan"),
        P(None, None, "chan"),
    )
    out_specs = P(("seq", "chan"), None, None)
    return jax.shard_map(
        on_device, mesh=mesh, in_specs=in_specs, out_specs=out_specs, check_vma=False
    )
```

```python
import functools

import jax
import jax.numpy as jnp
from jax import lax
from jax.experimental import pallas as pl
from jax.experimental.pallas import tpu as pltpu
from jax.sharding import PartitionSpec as P

block = 256
per_group = 16


def shifted(value, axis, steps):
    count = lax.axis_size(axis)
    leading, last = (max(0, -steps), min(count, count - steps))
    return lax.ppermute(value, axis, [(source, source + steps) for source in range(leading, last)])


def correlate_kernel(x_ref, h_ref, o_ref, acc_ref, rows_ref):
    tokens = x_ref.shape[1]
    blocks = tokens // block
    for index in range(blocks):
        rows_ref[per_group * index : per_group * (index + 1), :] = x_ref[:, block * index : block * (index + 1)]
    acc_ref[...] = jnp.zeros(acc_ref.shape, acc_ref.dtype)
    for lag_block in range(blocks):
        start = tokens - block * (lag_block + 1)
        window = h_ref[0, :, start : start + 2 * block]
        spread = jnp.broadcast_to(window, (block, 2 * block))
        rolled = pltpu.roll(spread, block + 1, 1, stride=1, stride_axis=0)
        band = rolled[:, :block].astype(jnp.bfloat16)
        rows = per_group * (blocks - lag_block)
        source = rows_ref[per_group * lag_block :, :]
        acc_ref[:rows, :] += jnp.dot(source, band, preferred_element_type=jnp.float32)
    for index in range(blocks):
        slab = acc_ref[per_group * index : per_group * (index + 1), :]
        first = block * index
        o_ref[first // o_ref.shape[2], :, pl.ds(first % o_ref.shape[2], block)] = slab.astype(o_ref.dtype)


def correlate(grads, taps, span):
    channels, tokens = grads.shape
    groups = taps.shape[1]
    blocks = tokens // block
    reversed_taps = taps.astype(jnp.float32).T[:, ::-1]
    padded = jnp.concatenate([reversed_taps, jnp.zeros((groups, block), jnp.float32)], 1)
    padded = padded.reshape(groups, 1, tokens + block)
    flops = 2 * groups * per_group * block * block * blocks * (blocks + 1) // 2
    return pl.pallas_call(
        correlate_kernel,
        out_shape=jax.ShapeDtypeStruct((tokens // span, channels, span), jnp.bfloat16),
        grid=(groups,),
        in_specs=[
            pl.BlockSpec((per_group, tokens), lambda g: (g, 0)),
            pl.BlockSpec((1, 1, tokens + block), lambda g: (g, 0, 0)),
        ],
        out_specs=pl.BlockSpec((tokens // span, per_group, span), lambda g: (0, g, 0)),
        scratch_shapes=[
            pltpu.VMEM((blocks * per_group, block), jnp.float32),
            pltpu.VMEM((blocks * per_group, block), jnp.bfloat16),
        ],
        cost_estimate=pl.CostEstimate(
            flops=flops, bytes_accessed=grads.size * 4 + padded.size * 4, transcendentals=0
        ),
    )(grads, padded)


def on_device(grad_out, qkv_saved, conv_saved, long_taps, short_taps):
    block_rows, channels = grad_out.shape
    out_wide = grad_out.astype(jnp.float32)
    query = qkv_saved[:, 0, :]
    key_part = qkv_saved[:, 1, :]
    value_part = qkv_saved[:, 2, :]
    grad_query = out_wide * conv_saved.astype(jnp.float32)
    grad_mixed = (out_wide * query.astype(jnp.float32)).astype(jnp.bfloat16)
    short_len = short_taps.shape[1]
    query_next = shifted(grad_query[: short_len - 1, None], "seq", -1)
    grad_mixed, query_next = lax.optimization_barrier((grad_mixed, query_next))
    mixed_cols = lax.all_to_all(grad_mixed.T, "seq", split_axis=0, concat_axis=1, tiled=True)
    taps_cols = lax.all_to_all(long_taps, "seq", split_axis=1, concat_axis=0, tiled=True)
    short_len = short_taps.shape[1]
    query_proj = short_filter(grad_query[:, None], short_taps[:1], block_rows, query_next)
    query_rows = spread_rows(query_proj, "chan")
    z_lanes = correlate(mixed_cols, taps_cols, block_rows)
    z_lanes, query_rows = lax.optimization_barrier((z_lanes, query_rows))
    z_rows = lax.all_to_all(z_lanes, "seq", split_axis=0, concat_axis=0, tiled=True)
    z_rows = z_rows.reshape(-1, block_rows)
    z_wide = z_rows.astype(jnp.float32)
    grad_key = z_wide * value_part.T.astype(jnp.float32)
    grad_value = z_wide * key_part.T.astype(jnp.float32)
    count = lax.axis_size("chan")
    out = jnp.zeros((block_rows // count, 3, count * channels), jnp.bfloat16)
    for source, piece in query_rows:
        out = lax.dynamic_update_slice(out, piece, (0, 0, source * channels))
    for plane, lanes in ((1, grad_key), (2, grad_value)):
        filtered = lane_filter(lanes, short_taps[plane])
        for source, piece in spread_lanes(filtered, "chan"):
            out = lax.dynamic_update_slice(out, piece.T[:, None, :], (0, plane, source * channels))
    return out


def lane_filter(lanes, taps):
    block_rows = lanes.shape[1]
    short_len = taps.shape[0]
    borrowed = shifted(lanes[:, : short_len - 1], "seq", -1)
    extended = jnp.concatenate([lanes, borrowed], 1)
    result = jnp.zeros_like(lanes)
    for lag_index in range(short_len):
        result = result + taps[lag_index][:, None] * extended[:, lag_index : lag_index + block_rows]
    return result.astype(jnp.bfloat16)


def spread_lanes(value, axis):
    count = lax.axis_size(axis)
    me = lax.axis_index(axis)
    width = value.shape[1] // count

    def lanes_for(index):
        return lax.dynamic_slice_in_dim(value, pl.multiple_of(index * width, width), width, 1)

    pieces = [(me, lanes_for(me))]
    for step in range(1, count):
        pairs = [(source, (source + step) % count) for source in range(count)]
        outgoing = lanes_for((me + step) % count)
        pieces.append(((me + count - step) % count, lax.ppermute(outgoing, axis, pairs)))
    return pieces


def spread_rows(value, axis):
    count = lax.axis_size(axis)
    me = lax.axis_index(axis)
    rows, planes, channels = value.shape
    chunks = value.reshape(count, rows // count, planes, channels)
    pieces = [(me, lax.dynamic_index_in_dim(chunks, me, 0, keepdims=False))]
    for step in range(1, count):
        outgoing = lax.dynamic_index_in_dim(chunks, (me + step) % count, 0, keepdims=False)
        pairs = [(source, (source + step) % count) for source in range(count)]
        pieces.append(((me + count - step) % count, lax.ppermute(outgoing, axis, pairs)))
    return pieces


def place_rows(parts, count, rows, channels):
    planes = sum(pieces[0][1].shape[1] for pieces in parts)
    out = jnp.zeros((rows, planes, count * channels), parts[0][0][1].dtype)
    plane = 0
    for pieces in parts:
        for source, piece in pieces:
            out = lax.dynamic_update_slice(out, piece, (0, plane, source * channels))
        plane += pieces[0][1].shape[1]
    return out


def short_filter(stacked, taps, block_rows, borrowed):
    short_len = taps.shape[1]
    extended = jnp.concatenate([stacked, borrowed], 0)
    result = jnp.zeros_like(stacked)
    for lag_index in range(short_len):
        result = result + taps[:, lag_index, :][None] * extended[lag_index : lag_index + block_rows]
    return result.astype(jnp.bfloat16)


def solution(mesh):
    in_specs = (
        P("seq", "chan"),
        P("seq", None, "chan"),
        P("seq", "chan"),
        P("seq", "chan"),
        P(None, None, "chan"),
    )
    out_specs = P(("seq", "chan"), None, None)
    return jax.shard_map(
        on_device, mesh=mesh, in_specs=in_specs, out_specs=out_specs, check_vma=False
    )
```
